256 devices in a mesh: dp: 8 (over y, z_lo), seq: 32 (over z_hi, x, core).
Axes of the slice: x: 4, y: 4, z: 8 (z_hi: 4, z_lo: 2; z = z_hi * 2 + z_lo), core: 2. Of those that a mesh axis runs over, the one named last changes fastest.
Arguments:
- tokens: bfloat16 [8, 256, 128, 512], P('dp', None, 'seq'), may hold values from -6 to 6
- patch_mask: int32 [8, 256, 128], P('dp', None, 'seq'), may hold values 0 or 1
- mask_token: float32 [512], replicated, may hold values from -6 to 6
- gain: float32 [512], replicated, may hold values from 0.1 to 1.9
- w_qkv: bfloat16 [512, 1536], replicated, may hold values from -0.25 to 0.25
- w_out: bfloat16 [512, 512], replicated, may hold values from -0.25 to 0.25
- block_ids: int32 [256], replicated, may hold values from 0 to 3, as said below
- temporal_mask: int32 [8, 8], replicated, may hold values from 0 to 1, as said below
- cotangent: bfloat16 [8, 256, 128, 512], P('dp', None, 'seq'), may hold values from -6 to 6
Outputs:
- layer_out: bfloat16 [8, 256, 128, 512], P('dp', None, 'seq')
- qkv_grad: float32 [1536, 512], P('seq')
- out_grad: float32 [512, 512], P('seq')
The draws below stay inside these ranges and needn't reach their ends.
Inputs may be any that keep to these rules, and one draw needn't show every extreme that they name: `block_ids`: each block id is held by exactly 64 electrodes. `temporal_mask`: every diagonal entry is 1.
All inputs are finite; a program needn't handle non-finite values. No bound on the sum of `patch_mask` on one device may be relied on, other than what follows from the above.
Results may differ from the reference program's by a relative error of at most 0.0092.
Values may be sent and summed in bfloat16 or wider, within the bound.
No kernel may reach another device: no remote copies, remote signals or barrier semaphores. Data moves between devices by JAX's collectives and lax.ppermute only.
A program may use at most 128 MiB of HBM per device.

```python
import jax
import jax.numpy as jnp
from jax import lax

E = 256
P_SIZE = 128
HEADS = 8
HEAD_DIM = 64
EB = 64
TB = 16
D = 512
RECS = 8


def draw_block_ids(key, part):
    return (jax.random.permutation(key, E) // EB).astype(jnp.int32)


def draw_temporal_mask(key, part):
    random_bits = jax.random.randint(key, (P_SIZE // TB, P_SIZE // TB), 0, 2).astype(jnp.int32)
    diagonal = jnp.eye(P_SIZE // TB, dtype=jnp.int32)
    return jnp.maximum(random_bits, diagonal).astype(jnp.int32)


def touch_ends(drawn, rng, least, largest):
    spot = [jax.random.randint(jax.random.fold_in(rng, axis), (), 0, length) for axis, length in enumerate(drawn.shape)]
    main_axis = drawn.shape.index(max(drawn.shape))
    neighbour = spot[:main_axis] + [(spot[main_axis] + 1) % drawn.shape[main_axis]] + spot[main_axis + 1:]
    return drawn.at[tuple(spot)].set(least).at[tuple(neighbour)].set(largest)


def raised(drawn, own_key, source, target, parts, factor):
    owner, partner = [(jnp.arange(drawn.shape[axis_at]) // (drawn.shape[axis_at] // parts)).reshape([-1 if axis == axis_at else 1 for axis in range(drawn.ndim)]) for axis_at in (source, target)]
    chosen = jax.random.permutation(own_key, parts)[partner]
    strong = (owner == chosen) | (owner == (partner + parts // 2) % parts)
    return jnp.where(strong, factor * drawn, drawn)


def level_of(rng, dims, cuts, low, top_value):
    def one(dim, parts):
        heights = jax.random.uniform(jax.random.fold_in(jax.random.fold_in(rng, 6), dim), (parts,), jnp.float32, low / len(cuts), top_value / len(cuts))
        return jnp.repeat(jnp.exp(heights), dims[dim] // parts).reshape((-1,) + (1,) * (len(dims) - dim - 1))

    factor_of = one(*cuts[0])
    for cut in cuts[1:]:
        factor_of = factor_of * one(*cut)
    return factor_of


def noise(key, shape, width, reach, shards=(), kind=jnp.bfloat16):
    array = width * jax.random.normal(key, shape, jnp.float32)
    if shards:
        array = array * level_of(key, shape, shards, -0.22, 0.18)
    return jnp.clip(array, -reach, reach).astype(kind)


def gaussian_with(own_key, extent, deviation, bound, pieces, heavy, kind=jnp.bfloat16):
    entries = deviation * jax.random.normal(own_key, extent, jnp.float32)
    if pieces:
        entries = entries * level_of(own_key, extent, pieces, -0.22, 0.18)
    return jnp.clip(raised(entries, jax.random.fold_in(own_key, 3), *heavy), -bound, bound).astype(kind)


def setup_inputs(seed: int = 0) -> dict:
    key_list = jax.random.split(jax.random.key(seed), 10)
    return {
        "tokens": noise(key_list[0], (RECS, E, P_SIZE, D), 1.0, 6.0, ((0, 8), (2, 32))),
        "patch_mask": touch_ends((jax.random.randint(key_list[1], (RECS, E, P_SIZE), 0, 2) < 1).astype(jnp.int32), jax.random.fold_in(key_list[1], 1), 0, 1),
        "mask_token": noise(key_list[2], (D,), 1.0, 6.0, (), jnp.float32),
        "gain": jnp.clip(1.0 + 0.18 * jax.random.normal(key_list[3], (D,), jnp.float32), 0.1, 1.9),
        "w_qkv": noise(key_list[4], (D, 3 * D), D ** -0.5, 0.25),
        "w_out": noise(key_list[5], (D, D), D ** -0.5, 0.25),
        "block_ids": draw_block_ids(jax.random.fold_in(key_list[9], 71), 0),
        "temporal_mask": draw_temporal_mask(jax.random.fold_in(key_list[9], 71), 0),
        "cotangent": gaussian_with(key_list[8], (RECS, E, P_SIZE, D), 1.0, 6.0, ((0, 8), (2, 32)), (2, 3, 32, 2.75)),
    }


NORM_EPS = 1e-05

def stored(tensor):
    return lax.optimization_barrier(tensor.astype(jnp.bfloat16))

def normed_input(tokens, patch_mask, mask_token, gain):
    masked = jnp.where(patch_mask[..., None] == 1, mask_token, tokens.astype(jnp.float32))
    row_mean = lax.optimization_barrier(jnp.mean(masked, axis=-1, keepdims=True))
    centred = masked - row_mean
    spread = lax.optimization_barrier(jnp.mean(centred * centred, axis=-1, keepdims=True))
    normed = stored(centred * lax.rsqrt(spread + NORM_EPS) * gain)
    return (masked, normed)

def forward_attend(queries, key_rows, values, allowed, factor):
    scores = jnp.einsum('anhd,amhd->ahnm', queries.astype(jnp.float32), key_rows.astype(jnp.float32)) * factor
    exponent = jnp.exp(scores) * allowed
    weights = exponent / lax.optimization_barrier(jnp.sum(exponent, axis=-1, keepdims=True))
    rounded = stored(weights)
    output = stored(jnp.einsum('ahnm,amhd->anhd', rounded.astype(jnp.float32), values.astype(jnp.float32)))
    return (output, weights, rounded)

def backward_attend(queries, key_rows, values, weights, rounded, grad_out, factor):
    grad_float = grad_out.astype(jnp.float32)
    grad_values = stored(jnp.einsum('ahnm,anhd->amhd', rounded.astype(jnp.float32), grad_float))
    grad_weights = jnp.einsum('anhd,amhd->ahnm', grad_float, values.astype(jnp.float32))
    inner_sum = lax.optimization_barrier(jnp.sum(grad_weights * weights, axis=-1, keepdims=True))
    grad_scores = stored(weights * (grad_weights - inner_sum)).astype(jnp.float32)
    grad_queries = stored(jnp.einsum('ahnm,amhd->anhd', grad_scores, key_rows.astype(jnp.float32)) * factor)
    grad_keys = stored(jnp.einsum('ahnm,anhd->amhd', grad_scores, queries.astype(jnp.float32)) * factor)
    return (grad_queries, grad_keys, grad_values)

def reference(tokens, patch_mask, mask_token, gain, w_qkv, w_out, block_ids, temporal_mask, cotangent):
    half_width = D // 2
    heads_half = HEADS // 2
    factor = HEAD_DIM ** (-0.5)
    same_block = (block_ids[:, None] == block_ids[None, :]).astype(jnp.float32)
    patch_block = (jnp.arange(P_SIZE) // TB).astype(jnp.int32)
    time_allowed = temporal_mask[patch_block][:, patch_block].astype(jnp.float32)

    def per_record(totals, inputs):
        record_tokens, record_mask, record_cot = inputs
        masked, normed = normed_input(record_tokens, record_mask, mask_token, gain)
        normed_flat = normed.reshape(E * P_SIZE, D)
        projected = stored(jnp.dot(normed_flat, w_qkv, preferred_element_type=jnp.float32))
        projected = projected.reshape(E, P_SIZE, 6, heads_half, HEAD_DIM)
        spatial = jnp.transpose(projected[:, :, :3], (1, 0, 2, 3, 4))
        space_out, space_weights, space_rounded = forward_attend(spatial[:, :, 0], spatial[:, :, 1], spatial[:, :, 2], same_block, factor)
        time_out, time_weights, time_rounded = forward_attend(projected[:, :, 3], projected[:, :, 4], projected[:, :, 5], time_allowed, factor)
        attended = jnp.concatenate([jnp.transpose(space_out, (1, 0, 2, 3)).reshape(E, P_SIZE, half_width), time_out.reshape(E, P_SIZE, half_width)], axis=-1)
        attended_flat = attended.reshape(E * P_SIZE, D)
        layer_out = (masked.reshape(E * P_SIZE, D) + jnp.dot(attended_flat, w_out, preferred_element_type=jnp.float32)).astype(jnp.bfloat16)
        cot_flat = record_cot.reshape(E * P_SIZE, D)
        out_grad = jnp.dot(cot_flat.T, attended_flat, preferred_element_type=jnp.float32)
        attended_grad = stored(jnp.dot(cot_flat, w_out.T, preferred_element_type=jnp.float32)).reshape(E, P_SIZE, D)
        space_grad = jnp.transpose(attended_grad[:, :, :half_width].reshape(E, P_SIZE, heads_half, HEAD_DIM), (1, 0, 2, 3))
        space_grads = backward_attend(spatial[:, :, 0], spatial[:, :, 1], spatial[:, :, 2], space_weights, space_rounded, space_grad, factor)
        time_grad = attended_grad[:, :, half_width:].reshape(E, P_SIZE, heads_half, HEAD_DIM)
        time_grads = backward_attend(projected[:, :, 3], projected[:, :, 4], projected[:, :, 5], time_weights, time_rounded, time_grad, factor)
        spatial_grad = jnp.transpose(jnp.stack(space_grads, axis=2), (1, 0, 2, 3, 4))
        temporal_grad = jnp.stack(time_grads, axis=2)
        projected_grad = jnp.concatenate([spatial_grad, temporal_grad], axis=2).reshape(E * P_SIZE, 3 * D)
        qkv_grad = jnp.dot(projected_grad.T, normed_flat, preferred_element_type=jnp.float32)
        return ((totals[0] + qkv_grad, totals[1] + out_grad), layer_out.reshape(E, P_SIZE, D))
    initial = (jnp.zeros((3 * D, D), jnp.float32), jnp.zeros((D, D), jnp.float32))
    totals, layer_out = lax.scan(per_record, initial, (tokens, patch_mask, cotangent))
    grad_scale = 1.0 / (RECS * E * P_SIZE) ** 0.5
    return (layer_out, totals[0] * grad_scale, totals[1] * grad_scale)
```

```python
import math

import jax
import jax.numpy as jnp
from jax import lax
from jax.sharding import PartitionSpec as P

P_SIZE = 128
HEADS = 8
HEAD_DIM = 64
EB = 64
TB = 16


NORM_EPS = 1e-05


def normed_input(tokens, patch_mask, mask_token, gain):
    masked = jnp.where(patch_mask[..., None] == 1, mask_token, tokens.astype(jnp.float32))
    row_mean = jnp.mean(masked, axis=-1, keepdims=True)
    centred = masked - row_mean
    spread = jnp.mean(centred * centred, axis=-1, keepdims=True)
    normed = (centred * lax.rsqrt(spread + NORM_EPS) * gain).astype(jnp.bfloat16)
    return (masked, normed)


def forward_attend(queries, key_rows, values, allowed, factor):
    scores = (
        jnp.einsum("anhd,amhd->ahnm", queries, key_rows, preferred_element_type=jnp.float32)
        * factor
    )
    exponent = jnp.exp(scores) * allowed
    weights = exponent / jnp.sum(exponent, axis=-1, keepdims=True)
    rounded = weights.astype(jnp.bfloat16)
    output = jnp.einsum(
        "ahnm,amhd->anhd", rounded, values, preferred_element_type=jnp.float32
    ).astype(jnp.bfloat16)
    return (output, weights, rounded)


def backward_attend(queries, key_rows, values, weights, rounded, grad_out, factor):
    grad_values = jnp.einsum(
        "ahnm,anhd->amhd", rounded, grad_out, preferred_element_type=jnp.float32
    ).astype(jnp.bfloat16)
    grad_weights = jnp.einsum(
        "anhd,amhd->ahnm", grad_out, values, preferred_element_type=jnp.float32
    )
    inner_sum = jnp.sum(grad_weights * weights, axis=-1, keepdims=True)
    grad_scores = (weights * (grad_weights - inner_sum)).astype(jnp.bfloat16)
    grad_queries = (
        jnp.einsum("ahnm,amhd->anhd", grad_scores, key_rows, preferred_element_type=jnp.float32)
        * factor
    ).astype(jnp.bfloat16)
    grad_keys = (
        jnp.einsum("ahnm,anhd->amhd", grad_scores, queries, preferred_element_type=jnp.float32)
        * factor
    ).astype(jnp.bfloat16)
    return (grad_queries, grad_keys, grad_values)


def to_blocks(tensor, block_order, block_size):
    record_count, electrodes, local_patches = tensor.shape[:3]
    trailing = tensor.shape[3:]
    picked = jnp.take(tensor, block_order, axis=1)
    picked = picked.reshape(
        (record_count, electrodes // block_size, block_size, local_patches) + trailing
    )
    picked = jnp.moveaxis(picked, 3, 2)
    return picked.reshape(
        (record_count * (electrodes // block_size) * local_patches, block_size) + trailing
    )


def from_blocks(tensor, inverse, record_count, electrodes, local_patches):
    block_size = tensor.shape[1]
    trailing = tensor.shape[2:]
    restored = tensor.reshape(
        (record_count, electrodes // block_size, local_patches, block_size) + trailing
    )
    restored = jnp.moveaxis(restored, 2, 3).reshape(
        (record_count, electrodes, local_patches) + trailing
    )
    return jnp.take(restored, inverse, axis=1)


def shards(tokens, patch_mask, mask_token, gain, w_qkv, w_out, block_ids, temporal_mask, cotangent):
    record_count, electrodes, local_patches, model_width = tokens.shape
    half_width = model_width // 2
    heads_half = HEADS // 2
    factor = HEAD_DIM ** (-0.5)
    block_order = jnp.argsort(block_ids, stable=True)
    inverse = jnp.argsort(block_order, stable=True)
    onehot = (jnp.arange(P_SIZE)[:, None] // TB == jnp.arange(P_SIZE // TB)[None, :]).astype(
        jnp.float32
    )
    time_allowed = jnp.dot(jnp.dot(onehot, temporal_mask.astype(jnp.float32)), onehot.T)
    same_block = jnp.ones((EB, EB), jnp.float32)
    masked, normed = normed_input(tokens, patch_mask, mask_token, gain)
    normed_flat = normed.reshape(-1, model_width)
    local_columns = 3 * model_width
    projected = jnp.dot(normed_flat, w_qkv, preferred_element_type=jnp.float32).astype(jnp.bfloat16)
    projected = projected.reshape(
        record_count, electrodes, local_patches, local_columns // half_width, heads_half, HEAD_DIM
    )
    spatial = to_blocks(projected[:, :, :, :3], block_order, EB)
    space_out, space_weights, space_rounded = forward_attend(
        spatial[:, :, 0], spatial[:, :, 1], spatial[:, :, 2], same_block, factor
    )
    time_part = projected[:, :, :, 3:].reshape(
        record_count, electrodes, local_patches, 3 * half_width
    )
    regrouped = lax.all_to_all(time_part, "seq", split_axis=1, concat_axis=2, tiled=True)
    items = regrouped.shape[0]
    owned = regrouped.shape[1]
    split_heads = regrouped.reshape(items * owned, P_SIZE, 3, heads_half, HEAD_DIM)
    time_out, time_weights, time_rounded = forward_attend(
        split_heads[:, :, 0], split_heads[:, :, 1], split_heads[:, :, 2], time_allowed, factor
    )
    time_out = time_out.reshape(items, owned, P_SIZE, half_width)
    time_back = lax.all_to_all(time_out, "seq", split_axis=2, concat_axis=1, tiled=True)
    space_back = from_blocks(space_out, inverse, record_count, electrodes, local_patches).reshape(
        record_count, electrodes, local_patches, half_width
    )
    attended = jnp.concatenate([space_back, time_back], axis=-1)
    attended_flat = attended.reshape(-1, model_width)
    layer_out = (
        masked.reshape(-1, model_width)
        + jnp.dot(attended_flat, w_out, preferred_element_type=jnp.float32)
    ).astype(jnp.bfloat16)
    layer_out = layer_out.reshape(tokens.shape)
    cot_flat = cotangent.reshape(-1, model_width)
    out_grad = jnp.einsum("tc,td->cd", cot_flat, attended_flat, preferred_element_type=jnp.float32)
    attended_grad = jnp.einsum(
        "td,cd->tc", cot_flat, w_out, preferred_element_type=jnp.float32
    ).astype(jnp.bfloat16)
    attended_grad = attended_grad.reshape(record_count, electrodes, local_patches, model_width)
    space_grad = to_blocks(
        attended_grad[..., :half_width].reshape(
            record_count, electrodes, local_patches, heads_half, HEAD_DIM
        ),
        block_order,
        EB,
    )
    space_grads = backward_attend(
        spatial[:, :, 0],
        spatial[:, :, 1],
        spatial[:, :, 2],
        space_weights,
        space_rounded,
        space_grad,
        factor,
    )
    spatial_grad = from_blocks(
        jnp.stack(space_grads, axis=2), inverse, record_count, electrodes, local_patches
    )
    spatial_grad = spatial_grad.reshape(-1, 3 * half_width)
    time_grad = lax.all_to_all(
        attended_grad[..., half_width:], "seq", split_axis=1, concat_axis=2, tiled=True
    )
    owned = time_grad.shape[1]
    split_heads = regrouped.reshape(record_count * owned, P_SIZE, 3, heads_half, HEAD_DIM)
    unused_out, time_weights, time_rounded = forward_attend(
        split_heads[:, :, 0], split_heads[:, :, 1], split_heads[:, :, 2], time_allowed, factor
    )
    time_grads = backward_attend(
        split_heads[:, :, 0],
        split_heads[:, :, 1],
        split_heads[:, :, 2],
        time_weights,
        time_rounded,
        time_grad.reshape(record_count * owned, P_SIZE, heads_half, HEAD_DIM),
        factor,
    )
    temporal_grad = jnp.stack(time_grads, axis=2).reshape(
        record_count, owned, P_SIZE, 3 * half_width
    )
    temporal_back = lax.all_to_all(
        temporal_grad, "seq", split_axis=2, concat_axis=1, tiled=True
    ).reshape(-1, 3 * half_width)
    projected_grad = jnp.concatenate([spatial_grad, temporal_back], axis=1)
    qkv_grad = jnp.einsum(
        "tc,td->cd", projected_grad, normed_flat, preferred_element_type=jnp.float32
    )
    groups = lax.axis_size("seq")
    grad_scale = 1.0 / math.sqrt(
        record_count * lax.axis_size("dp") * electrodes * local_patches * groups
    )
    rows_qkv = qkv_grad.shape[0] // groups
    rows_out = model_width // groups
    stacked = jnp.concatenate(
        [
            qkv_grad.reshape(groups, rows_qkv, model_width),
            out_grad.reshape(groups, rows_out, model_width),
        ],
        axis=1,
    )
    share = lax.psum_scatter(stacked, "seq", scatter_dimension=0, tiled=True)
    share = lax.psum(share, "dp").reshape(rows_qkv + rows_out, model_width)
    return (layer_out, share[:rows_qkv] * grad_scale, share[rows_qkv:] * grad_scale)


def solution(mesh):
    return jax.shard_map(
        shards,
        mesh=mesh,
        in_specs=(
            P("dp", None, "seq", None),
            P("dp", None, "seq"),
            P(),
            P(),
            P(),
            P(),
            P(),
            P(),
            P("dp", None, "seq", None),
        ),
        out_specs=(P("dp", None, "seq", None), P("seq", None), P("seq", None)),
        check_vma=False,
    )
```

```python
import math

import jax
import jax.numpy as jnp
from jax import lax
from jax.sharding import PartitionSpec as P

P_SIZE = 128
HEADS = 8
HEAD_DIM = 64
EB = 64
TB = 16


NORM_EPS = 1e-05


def normed_input(tokens, patch_mask, mask_token, gain):
    masked = jnp.where(patch_mask[..., None] == 1, mask_token, tokens.astype(jnp.float32))
    row_mean = jnp.mean(masked, axis=-1, keepdims=True)
    centred = masked - row_mean
    spread = jnp.mean(centred * centred, axis=-1, keepdims=True)
    normed = (centred * lax.rsqrt(spread + NORM_EPS) * gain).astype(jnp.bfloat16)
    return (masked, normed)


def forward_attend(queries, key_rows, values, allowed, factor):
    scores = (
        jnp.einsum("anhd,amhd->ahnm", queries, key_rows, preferred_element_type=jnp.float32)
        * factor
    )
    exponent = jnp.exp(scores) * allowed
    weights = exponent / jnp.sum(exponent, axis=-1, keepdims=True)
    rounded = weights.astype(jnp.bfloat16)
    output = jnp.einsum(
        "ahnm,amhd->anhd", rounded, values, preferred_element_type=jnp.float32
    ).astype(jnp.bfloat16)
    return (output, weights, rounded)


def backward_attend(queries, key_rows, values, weights, rounded, grad_out, factor):
    grad_values = jnp.einsum(
        "ahnm,anhd->amhd", rounded, grad_out, preferred_element_type=jnp.float32
    ).astype(jnp.bfloat16)
    grad_weights = jnp.einsum(
        "anhd,amhd->ahnm", grad_out, values, preferred_element_type=jnp.float32
    )
    inner_sum = jnp.sum(grad_weights * weights, axis=-1, keepdims=True)
    grad_scores = (weights * (grad_weights - inner_sum)).astype(jnp.bfloat16)
    grad_queries = (
        jnp.einsum("ahnm,amhd->anhd", grad_scores, key_rows, preferred_element_type=jnp.float32)
        * factor
    ).astype(jnp.bfloat16)
    grad_keys = (
        jnp.einsum("ahnm,anhd->amhd", grad_scores, queries, preferred_element_type=jnp.float32)
        * factor
    ).astype(jnp.bfloat16)
    return (grad_queries, grad_keys, grad_values)


def to_blocks(tensor, block_order, block_size):
    record_count, electrodes, local_patches = tensor.shape[:3]
    trailing = tensor.shape[3:]
    picked = jnp.take(tensor, block_order, axis=1)
    picked = picked.reshape(
        (record_count, electrodes // block_size, block_size, local_patches) + trailing
    )
    picked = jnp.moveaxis(picked, 3, 2)
    return picked.reshape(
        (record_count * (electrodes // block_size) * local_patches, block_size) + trailing
    )


def from_blocks(tensor, inverse, record_count, electrodes, local_patches):
    block_size = tensor.shape[1]
    trailing = tensor.shape[2:]
    restored = tensor.reshape(
        (record_count, electrodes // block_size, local_patches, block_size) + trailing
    )
    restored = jnp.moveaxis(restored, 2, 3).reshape(
        (record_count, electrodes, local_patches) + trailing
    )
    return jnp.take(restored, inverse, axis=1)


def shards(tokens, patch_mask, mask_token, gain, w_qkv, w_out, block_ids, temporal_mask, cotangent):
    record_count, electrodes, local_patches, model_width = tokens.shape
    half_width = model_width // 2
    heads_half = HEADS // 2
    factor = HEAD_DIM ** (-0.5)
    block_order = jnp.argsort(block_ids, stable=True)
    inverse = jnp.argsort(block_order, stable=True)
    onehot = (jnp.arange(P_SIZE)[:, None] // TB == jnp.arange(P_SIZE // TB)[None, :]).astype(
        jnp.float32
    )
    time_allowed = jnp.dot(jnp.dot(onehot, temporal_mask.astype(jnp.float32)), onehot.T)
    same_block = jnp.ones((EB, EB), jnp.float32)
    masked, normed = normed_input(tokens, patch_mask, mask_token, gain)
    normed_flat = normed.reshape(-1, model_width)
    local_columns = 3 * model_width
    projected = jnp.dot(normed_flat, w_qkv, preferred_element_type=jnp.float32).astype(jnp.bfloat16)
    projected = projected.reshape(
        record_count, electrodes, local_patches, local_columns // half_width, heads_half, HEAD_DIM
    )
    spatial = to_blocks(projected[:, :, :, :3], block_order, EB)
    space_out, space_weights, space_rounded = forward_attend(
        spatial[:, :, 0], spatial[:, :, 1], spatial[:, :, 2], same_block, factor
    )
    time_part = projected[:, :, :, 3:].reshape(
        record_count, electrodes, local_patches, 3 * half_width
    )
    regrouped = lax.all_to_all(time_part, "seq", split_axis=1, concat_axis=2, tiled=True)
    items = regrouped.shape[0]
    owned = regrouped.shape[1]
    split_heads = regrouped.reshape(items * owned, P_SIZE, 3, heads_half, HEAD_DIM)
    time_out, time_weights, time_rounded = forward_attend(
        split_heads[:, :, 0], split_heads[:, :, 1], split_heads[:, :, 2], time_allowed, factor
    )
    time_out = time_out.reshape(items, owned, P_SIZE, half_width)
    time_back = lax.all_to_all(time_out, "seq", split_axis=2, concat_axis=1, tiled=True)
    space_back = from_blocks(space_out, inverse, record_count, electrodes, local_patches).reshape(
        record_count, electrodes, local_patches, half_width
    )
    attended = jnp.concatenate([space_back, time_back], axis=-1)
    attended_flat = attended.reshape(-1, model_width)
    layer_out = (
        masked.reshape(-1, model_width)
        + jnp.dot(attended_flat, w_out, preferred_element_type=jnp.float32)
    ).astype(jnp.bfloat16)
    layer_out = layer_out.reshape(tokens.shape)
    cot_flat = cotangent.reshape(-1, model_width)
    out_grad = jnp.einsum("tc,td->cd", cot_flat, attended_flat, preferred_element_type=jnp.float32)
    attended_grad = jnp.einsum(
        "td,cd->tc", cot_flat, w_out, preferred_element_type=jnp.float32
    ).astype(jnp.bfloat16)
    attended_grad = attended_grad.reshape(record_count, electrodes, local_patches, model_width)
    space_grad = to_blocks(
        attended_grad[..., :half_width].reshape(
            record_count, electrodes, local_patches, heads_half, HEAD_DIM
        ),
        block_order,
        EB,
    )
    space_grads = backward_attend(
        spatial[:, :, 0],
        spatial[:, :, 1],
        spatial[:, :, 2],
        space_weights,
        space_rounded,
        space_grad,
        factor,
    )
    spatial_grad = from_blocks(
        jnp.stack(space_grads, axis=2), inverse, record_count, electrodes, local_patches
    )
    spatial_grad = spatial_grad.reshape(-1, 3 * half_width)
    time_grad = lax.all_to_all(
        attended_grad[..., half_width:], "seq", split_axis=1, concat_axis=2, tiled=True
    )
    owned = time_grad.shape[1]
    split_heads = regrouped.reshape(record_count * owned, P_SIZE, 3, heads_half, HEAD_DIM)
    unused_out, time_weights, time_rounded = forward_attend(
        split_heads[:, :, 0], split_heads[:, :, 1], split_heads[:, :, 2], time_allowed, factor
    )
    time_grads = backward_attend(
        split_heads[:, :, 0],
        split_heads[:, :, 1],
        split_heads[:, :, 2],
        time_weights,
        time_rounded,
        time_grad.reshape(record_count * owned, P_SIZE, heads_half, HEAD_DIM),
        factor,
    )
    temporal_grad = jnp.stack(time_grads, axis=2).reshape(
        record_count, owned, P_SIZE, 3 * half_width
    )
    temporal_back = lax.all_to_all(
        temporal_grad, "seq", split_axis=2, concat_axis=1, tiled=True
    ).reshape(-1, 3 * half_width)
    projected_grad = jnp.concatenate([spatial_grad, temporal_back], axis=1)
    qkv_grad = jnp.einsum(
        "tc,td->cd", projected_grad, normed_flat, preferred_element_type=jnp.float32
    )
    groups = lax.axis_size("seq")
    grad_scale = 1.0 / math.sqrt(
        record_count * lax.axis_size("dp") * electrodes * local_patches * groups
    )
    rows_qkv = qkv_grad.shape[0] // groups
    rows_out = model_width // groups
    stacked = jnp.concatenate(
        [
            qkv_grad.reshape(groups, rows_qkv, model_width),
            out_grad.reshape(groups, rows_out, model_width),
        ],
        axis=1,
    )
    gathered = lax.all_to_all(stacked, "seq", split_axis=0, concat_axis=0, tiled=True)
    share = jnp.sum(gathered, axis=0)
    members = lax.axis_size("dp")
    pieces = share.reshape(members, (rows_qkv + rows_out) // members, model_width)
    pieces = lax.all_to_all(pieces, "dp", split_axis=0, concat_axis=0, tiled=True)
    piece = jnp.sum(pieces, axis=0, keepdims=True)
    spread = jnp.broadcast_to(piece, pieces.shape)
    share = lax.all_to_all(spread, "dp", split_axis=0, concat_axis=0, tiled=True)
    share = share.reshape(rows_qkv + rows_out, model_width)
    return (layer_out, share[:rows_qkv] * grad_scale, share[rows_qkv:] * grad_scale)


def solution(mesh):
    return jax.shard_map(
        shards,
        mesh=mesh,
        in_specs=(
            P("dp", None, "seq", None),
            P("dp", None, "seq"),
            P(),
            P(),
            P(),
            P(),
            P(),
            P(),
            P("dp", None, "seq", None),
        ),
        out_specs=(P("dp", None, "seq", None), P("seq", None), P("seq", None)),
        check_vma=False,
    )
```

```python
import math

import jax
import jax.numpy as jnp
from jax import lax
from jax.sharding import PartitionSpec as P

P_SIZE = 128
HEADS = 8
HEAD_DIM = 64
EB = 64
TB = 16


NORM_EPS = 1e-05


def normed_input(tokens, patch_mask, mask_token, gain):
    masked = jnp.where(patch_mask[..., None] == 1, mask_token, tokens.astype(jnp.float32))
    row_mean = jnp.mean(masked, axis=-1, keepdims=True)
    centred = masked - row_mean
    spread = jnp.mean(centred * centred, axis=-1, keepdims=True)
    normed = (centred * lax.rsqrt(spread + NORM_EPS) * gain).astype(jnp.bfloat16)
    return (masked, normed)


def forward_attend(queries, key_rows, values, allowed, factor):
    scores = (
        jnp.einsum("anhd,amhd->ahnm", queries, key_rows, preferred_element_type=jnp.float32)
        * factor
    )
    exponent = jnp.exp(scores) * allowed
    weights = exponent / jnp.sum(exponent, axis=-1, keepdims=True)
    rounded = weights.astype(jnp.bfloat16)
    output = jnp.einsum(
        "ahnm,amhd->anhd", rounded, values, preferred_element_type=jnp.float32
    ).astype(jnp.bfloat16)
    return (output, weights, rounded)


def backward_attend(queries, key_rows, values, weights, rounded, grad_out, factor):
    grad_values = jnp.einsum(
        "ahnm,anhd->amhd", rounded, grad_out, preferred_element_type=jnp.float32
    ).astype(jnp.bfloat16)
    grad_weights = jnp.einsum(
        "anhd,amhd->ahnm", grad_out, values, preferred_element_type=jnp.float32
    )
    inner_sum = jnp.sum(grad_weights * weights, axis=-1, keepdims=True)
    grad_scores = (weights * (grad_weights - inner_sum)).astype(jnp.bfloat16)
    grad_queries = (
        jnp.einsum("ahnm,amhd->anhd", grad_scores, key_rows, preferred_element_type=jnp.float32)
        * factor
    ).astype(jnp.bfloat16)
    grad_keys = (
        jnp.einsum("ahnm,anhd->amhd", grad_scores, queries, preferred_element_type=jnp.float32)
        * factor
    ).astype(jnp.bfloat16)
    return (grad_queries, grad_keys, grad_values)


def to_blocks(tensor, block_order, block_size):
    record_count, electrodes, local_patches = tensor.shape[:3]
    trailing = tensor.shape[3:]
    picked = jnp.take(tensor, block_order, axis=1)
    picked = picked.reshape(
        (record_count, electrodes // block_size, block_size, local_patches) + trailing
    )
    picked = jnp.moveaxis(picked, 3, 2)
    return picked.reshape(
        (record_count * (electrodes // block_size) * local_patches, block_size) + trailing
    )


def from_blocks(tensor, inverse, record_count, electrodes, local_patches):
    block_size = tensor.shape[1]
    trailing = tensor.shape[2:]
    restored = tensor.reshape(
        (record_count, electrodes // block_size, local_patches, block_size) + trailing
    )
    restored = jnp.moveaxis(restored, 2, 3).reshape(
        (record_count, electrodes, local_patches) + trailing
    )
    return jnp.take(restored, inverse, axis=1)


def shards(tokens, patch_mask, mask_token, gain, w_qkv, w_out, block_ids, temporal_mask, cotangent):
    record_count, electrodes, local_patches, model_width = tokens.shape
    half_width = model_width // 2
    heads_half = HEADS // 2
    factor = HEAD_DIM ** (-0.5)
    block_order = jnp.argsort(block_ids, stable=True)
    inverse = jnp.argsort(block_order, stable=True)
    onehot = (jnp.arange(P_SIZE)[:, None] // TB == jnp.arange(P_SIZE // TB)[None, :]).astype(
        jnp.float32
    )
    time_allowed = jnp.dot(jnp.dot(onehot, temporal_mask.astype(jnp.float32)), onehot.T)
    same_block = jnp.ones((EB, EB), jnp.float32)
    masked, normed = normed_input(tokens, patch_mask, mask_token, gain)
    normed_flat = normed.reshape(-1, model_width)
    local_columns = 3 * model_width
    projected = jnp.dot(normed_flat, w_qkv, preferred_element_type=jnp.float32).astype(jnp.bfloat16)
    projected = projected.reshape(
        record_count, electrodes, local_patches, local_columns // half_width, heads_half, HEAD_DIM
    )
    spatial = to_blocks(projected[:, :, :, :3], block_order, EB)
    space_out, space_weights, space_rounded = forward_attend(
        spatial[:, :, 0], spatial[:, :, 1], spatial[:, :, 2], same_block, factor
    )
    time_part = projected[:, :, :, 3:].reshape(
        record_count, electrodes, local_patches, 3 * half_width
    )
    regrouped = lax.all_to_all(time_part, "seq", split_axis=1, concat_axis=2, tiled=True)
    items = regrouped.shape[0]
    owned = regrouped.shape[1]
    split_heads = regrouped.reshape(items * owned, P_SIZE, 3, heads_half, HEAD_DIM)
    time_out, time_weights, time_rounded = forward_attend(
        split_heads[:, :, 0], split_heads[:, :, 1], split_heads[:, :, 2], time_allowed, factor
    )
    time_out = time_out.reshape(items, owned, P_SIZE, half_width)
    time_back = lax.all_to_all(time_out, "seq", split_axis=2, concat_axis=1, tiled=True)
    space_back = from_blocks(space_out, inverse, record_count, electrodes, local_patches).reshape(
        record_count, electrodes, local_patches, half_width
    )
    attended = jnp.concatenate([space_back, time_back], axis=-1)
    attended_flat = attended.reshape(-1, model_width)
    layer_out = (
        masked.reshape(-1, model_width)
        + jnp.dot(attended_flat, w_out, preferred_element_type=jnp.float32)
    ).astype(jnp.bfloat16)
    layer_out = layer_out.reshape(tokens.shape)
    cot_flat = cotangent.reshape(-1, model_width)
    out_grad = jnp.einsum("tc,td->cd", cot_flat, attended_flat, preferred_element_type=jnp.float32)
    attended_grad = jnp.einsum(
        "td,cd->tc", cot_flat, w_out, preferred_element_type=jnp.float32
    ).astype(jnp.bfloat16)
    attended_grad = attended_grad.reshape(record_count, electrodes, local_patches, model_width)
    space_grad = to_blocks(
        attended_grad[..., :half_width].reshape(
            record_count, electrodes, local_patches, heads_half, HEAD_DIM
        ),
        block_order,
        EB,
    )
    space_grads = backward_attend(
        spatial[:, :, 0],
        spatial[:, :, 1],
        spatial[:, :, 2],
        space_weights,
        space_rounded,
        space_grad,
        factor,
    )
    spatial_grad = from_blocks(
        jnp.stack(space_grads, axis=2), inverse, record_count, electrodes, local_patches
    )
    spatial_grad = spatial_grad.reshape(-1, 3 * half_width)
    time_grad = lax.all_to_all(
        attended_grad[..., half_width:], "seq", split_axis=1, concat_axis=2, tiled=True
    )
    owned = time_grad.shape[1]
    split_heads = regrouped.reshape(record_count * owned, P_SIZE, 3, heads_half, HEAD_DIM)
    unused_out, time_weights, time_rounded = forward_attend(
        split_heads[:, :, 0], split_heads[:, :, 1], split_heads[:, :, 2], time_allowed, factor
    )
    time_grads = backward_attend(
        split_heads[:, :, 0],
        split_heads[:, :, 1],
        split_heads[:, :, 2],
        time_weights,
        time_rounded,
        time_grad.reshape(record_count * owned, P_SIZE, heads_half, HEAD_DIM),
        factor,
    )
    temporal_grad = jnp.stack(time_grads, axis=2).reshape(
        record_count, owned, P_SIZE, 3 * half_width
    )
    temporal_back = lax.all_to_all(
        temporal_grad, "seq", split_axis=2, concat_axis=1, tiled=True
    ).reshape(-1, 3 * half_width)
    projected_grad = jnp.concatenate([spatial_grad, temporal_back], axis=1)
    qkv_grad = jnp.einsum(
        "tc,td->cd", projected_grad, normed_flat, preferred_element_type=jnp.float32
    )
    groups = lax.axis_size("seq")
    grad_scale = 1.0 / math.sqrt(
        record_count * lax.axis_size("dp") * electrodes * local_patches * groups
    )
    rows_qkv = qkv_grad.shape[0] // groups
    rows_out = model_width // groups
    stacked = jnp.concatenate(
        [
            qkv_grad.reshape(groups, rows_qkv, model_width),
            out_grad.reshape(groups, rows_out, model_width),
        ],
        axis=1,
    )
    share = reduce_share(stacked, groups, lax.axis_size("dp"))
    return (layer_out, share[:rows_qkv] * grad_scale, share[rows_qkv:] * grad_scale)


def seq_perm(groups, move):
    return [(index, move(index)) for index in range(groups)]


def ring_reduce(own, position, size, forward, backward):
    half = own.shape[2] // 2
    ahead, behind = own[:, :, :half], own[:, :, half:]

    def pick(values, offset):
        return lax.dynamic_index_in_dim(values, (position + offset) % size, 0, keepdims=False)

    sent_ahead = pick(ahead, size - 1)
    sent_behind = pick(behind, 1)
    for step in range(size - 1):
        got_ahead = lax.ppermute(sent_ahead, "seq", forward)
        got_behind = lax.ppermute(sent_behind, "seq", backward)
        sent_ahead = got_ahead + pick(ahead, 2 * size - 2 - step)
        sent_behind = got_behind + pick(behind, 2 + step)
    return jnp.concatenate([sent_ahead, sent_behind], axis=1)


def reduce_share(stacked, groups, members):
    cores, xs = 2, 4
    zs = groups // (cores * xs)
    rows, width = stacked.shape[1:]
    index = lax.axis_index("seq")
    core = index % cores
    x_at = (index // cores) % xs
    z_at = index // (cores * xs)
    blocks = stacked.reshape(zs, xs, cores, rows, width)
    keep = lax.dynamic_index_in_dim(blocks, core, 2, keepdims=False)
    send = lax.dynamic_index_in_dim(blocks, 1 - core, 2, keepdims=False)
    summed = keep + lax.ppermute(send, "seq", seq_perm(groups, lambda i: i ^ 1))

    def x_move(step):
        def move(i):
            z, x, c = i // (cores * xs), (i // cores) % xs, i % cores
            return (z * xs + (x + step) % xs) * cores + c
        return seq_perm(groups, move)

    def z_move(step):
        def move(i):
            z, rest = i // (cores * xs), i % (cores * xs)
            return ((z + step) % zs) * cores * xs + rest
        return seq_perm(groups, move)

    by_x = jnp.swapaxes(summed, 0, 1)
    summed = ring_reduce(by_x, x_at, xs, x_move(1), x_move(xs - 1))
    summed = ring_reduce(summed[:, None], z_at, zs, z_move(1), z_move(zs - 1))[0]
    member = lax.axis_index("dp")
    bit = 1
    while bit < members:
        pairs = [(i, i ^ bit) for i in range(members)]
        summed = summed + lax.ppermute(summed, "dp", pairs)
        bit *= 2
    return summed


def solution(mesh):
    return jax.shard_map(
        shards,
        mesh=mesh,
        in_specs=(
            P("dp", None, "seq", None),
            P("dp", None, "seq"),
            P(),
            P(),
            P(),
            P(),
            P(),
            P(),
            P("dp", None, "seq", None),
        ),
        out_specs=(P("dp", None, "seq", None), P("seq", None), P("seq", None)),
        check_vma=False,
    )
```

```python
import math

import jax
import jax.numpy as jnp
from jax import lax
from jax.sharding import PartitionSpec as P

P_SIZE = 128
HEADS = 8
HEAD_DIM = 64
EB = 64
TB = 16


NORM_EPS = 1e-05


def normed_input(tokens, patch_mask, mask_token, gain):
    masked = jnp.where(patch_mask[..., None] == 1, mask_token, tokens.astype(jnp.float32))
    row_mean = jnp.mean(masked, axis=-1, keepdims=True)
    centred = masked - row_mean
    spread = jnp.mean(centred * centred, axis=-1, keepdims=True)
    normed = (centred * lax.rsqrt(spread + NORM_EPS) * gain).astype(jnp.bfloat16)
    return (masked, normed)


def forward_attend(queries, key_rows, values, allowed, factor):
    scores = (
        jnp.einsum("anhd,amhd->ahnm", queries, key_rows, preferred_element_type=jnp.float32)
        * factor
    )
    exponent = jnp.exp(scores) * allowed
    weights = exponent / jnp.sum(exponent, axis=-1, keepdims=True)
    rounded = weights.astype(jnp.bfloat16)
    output = jnp.einsum(
        "ahnm,amhd->anhd", rounded, values, preferred_element_type=jnp.float32
    ).astype(jnp.bfloat16)
    return (output, weights, rounded)


def backward_attend(queries, key_rows, values, weights, rounded, grad_out, factor):
    grad_values = jnp.einsum(
        "ahnm,anhd->amhd", rounded, grad_out, preferred_element_type=jnp.float32
    ).astype(jnp.bfloat16)
    grad_weights = jnp.einsum(
        "anhd,amhd->ahnm", grad_out, values, preferred_element_type=jnp.float32
    )
    inner_sum = jnp.sum(grad_weights * weights, axis=-1, keepdims=True)
    grad_scores = (weights * (grad_weights - inner_sum)).astype(jnp.bfloat16)
    grad_queries = (
        jnp.einsum("ahnm,amhd->anhd", grad_scores, key_rows, preferred_element_type=jnp.float32)
        * factor
    ).astype(jnp.bfloat16)
    grad_keys = (
        jnp.einsum("ahnm,anhd->amhd", grad_scores, queries, preferred_element_type=jnp.float32)
        * factor
    ).astype(jnp.bfloat16)
    return (grad_queries, grad_keys, grad_values)


def to_blocks(tensor, block_order, block_size):
    record_count, electrodes, local_patches = tensor.shape[:3]
    trailing = tensor.shape[3:]
    picked = jnp.take(tensor, block_order, axis=1)
    picked = picked.reshape(
        (record_count, electrodes // block_size, block_size, local_patches) + trailing
    )
    picked = jnp.moveaxis(picked, 3, 2)
    return picked.reshape(
        (record_count * (electrodes // block_size) * local_patches, block_size) + trailing
    )


def from_blocks(tensor, inverse, record_count, electrodes, local_patches):
    block_size = tensor.shape[1]
    trailing = tensor.shape[2:]
    restored = tensor.reshape(
        (record_count, electrodes // block_size, local_patches, block_size) + trailing
    )
    restored = jnp.moveaxis(restored, 2, 3).reshape(
        (record_count, electrodes, local_patches) + trailing
    )
    return jnp.take(restored, inverse, axis=1)


def shards(tokens, patch_mask, mask_token, gain, w_qkv, w_out, block_ids, temporal_mask, cotangent):
    record_count, electrodes, local_patches, model_width = tokens.shape
    half_width = model_width // 2
    heads_half = HEADS // 2
    factor = HEAD_DIM ** (-0.5)
    onehot = (jnp.arange(P_SIZE)[:, None] // TB == jnp.arange(P_SIZE // TB)[None, :]).astype(
        jnp.float32
    )
    time_allowed = jnp.dot(jnp.dot(onehot, temporal_mask.astype(jnp.float32)), onehot.T)
    same_block = (block_ids[:, None] == block_ids[None, :]).astype(jnp.float32)
    masked, normed = normed_input(tokens, patch_mask, mask_token, gain)
    normed_flat = normed.reshape(-1, model_width)
    local_columns = 3 * model_width
    projected = jnp.dot(normed_flat, w_qkv, preferred_element_type=jnp.float32).astype(jnp.bfloat16)
    projected = projected.reshape(
        record_count, electrodes, local_patches, local_columns // half_width, heads_half, HEAD_DIM
    )
    spatial = jnp.transpose(projected[0, :, :, :3], (1, 0, 2, 3, 4))
    space_out, space_weights, space_rounded = forward_attend(
        spatial[:, :, 0], spatial[:, :, 1], spatial[:, :, 2], same_block, factor
    )
    time_part = projected[:, :, :, 3:].reshape(
        record_count, electrodes, local_patches, 3 * half_width
    )
    regrouped = lax.all_to_all(time_part, "seq", split_axis=1, concat_axis=2, tiled=True)
    items = regrouped.shape[0]
    owned = regrouped.shape[1]
    split_heads = regrouped.reshape(items * owned, P_SIZE, 3, heads_half, HEAD_DIM)
    time_out, time_weights, time_rounded = forward_attend(
        split_heads[:, :, 0], split_heads[:, :, 1], split_heads[:, :, 2], time_allowed, factor
    )
    time_out = time_out.reshape(items, owned, P_SIZE, half_width)
    time_back = lax.all_to_all(time_out, "seq", split_axis=2, concat_axis=1, tiled=True)
    space_back = jnp.transpose(space_out, (1, 0, 2, 3)).reshape(
        record_count, electrodes, local_patches, half_width
    )
    attended = jnp.concatenate([space_back, time_back], axis=-1)
    attended_flat = attended.reshape(-1, model_width)
    layer_out = (
        masked.reshape(-1, model_width)
        + jnp.dot(attended_flat, w_out, preferred_element_type=jnp.float32)
    ).astype(jnp.bfloat16)
    layer_out = layer_out.reshape(tokens.shape)
    cot_flat = cotangent.reshape(-1, model_width)
    out_grad = jnp.einsum("tc,td->cd", cot_flat, attended_flat, preferred_element_type=jnp.float32)
    attended_grad = jnp.einsum(
        "td,cd->tc", cot_flat, w_out, preferred_element_type=jnp.float32
    ).astype(jnp.bfloat16)
    attended_grad = attended_grad.reshape(record_count, electrodes, local_patches, model_width)
    space_grad = jnp.transpose(
        attended_grad[0, :, :, :half_width].reshape(electrodes, local_patches, heads_half, HEAD_DIM),
        (1, 0, 2, 3),
    )
    space_grads = backward_attend(
        spatial[:, :, 0],
        spatial[:, :, 1],
        spatial[:, :, 2],
        space_weights,
        space_rounded,
        space_grad,
        factor,
    )
    spatial_grad = jnp.transpose(jnp.stack(space_grads, axis=2), (1, 0, 2, 3, 4))
    spatial_grad = spatial_grad.reshape(-1, 3 * half_width)
    time_grad = lax.all_to_all(
        attended_grad[..., half_width:], "seq", split_axis=1, concat_axis=2, tiled=True
    )
    owned = time_grad.shape[1]
    split_heads = regrouped.reshape(record_count * owned, P_SIZE, 3, heads_half, HEAD_DIM)
    unused_out, time_weights, time_rounded = forward_attend(
        split_heads[:, :, 0], split_heads[:, :, 1], split_heads[:, :, 2], time_allowed, factor
    )
    time_grads = backward_attend(
        split_heads[:, :, 0],
        split_heads[:, :, 1],
        split_heads[:, :, 2],
        time_weights,
        time_rounded,
        time_grad.reshape(record_count * owned, P_SIZE, heads_half, HEAD_DIM),
        factor,
    )
    temporal_grad = jnp.stack(time_grads, axis=2).reshape(
        record_count, owned, P_SIZE, 3 * half_width
    )
    temporal_back = lax.all_to_all(
        temporal_grad, "seq", split_axis=2, concat_axis=1, tiled=True
    ).reshape(-1, 3 * half_width)
    projected_grad = jnp.concatenate([spatial_grad, temporal_back], axis=1)
    qkv_grad = jnp.einsum(
        "tc,td->cd", projected_grad, normed_flat, preferred_element_type=jnp.float32
    )
    groups = lax.axis_size("seq")
    grad_scale = 1.0 / math.sqrt(
        record_count * lax.axis_size("dp") * electrodes * local_patches * groups
    )
    rows_qkv = qkv_grad.shape[0] // groups
    rows_out = model_width // groups
    stacked = jnp.concatenate(
        [
            qkv_grad.reshape(groups, rows_qkv, model_width),
            out_grad.reshape(groups, rows_out, model_width),
        ],
        axis=1,
    )
    share = reduce_share(stacked, groups, lax.axis_size("dp"))
    return (layer_out, share[:rows_qkv] * grad_scale, share[rows_qkv:] * grad_scale)


def seq_perm(groups, move):
    return [(index, move(index)) for index in range(groups)]


def ring_reduce(own, position, size, forward, backward):
    half = own.shape[2] // 2
    ahead, behind = own[:, :, :half], own[:, :, half:]

    def pick(values, offset):
        return lax.dynamic_index_in_dim(values, (position + offset) % size, 0, keepdims=False)

    sent_ahead = pick(ahead, size - 1)
    sent_behind = pick(behind, 1)
    for step in range(size - 1):
        got_ahead = lax.ppermute(sent_ahead, "seq", forward)
        got_behind = lax.ppermute(sent_behind, "seq", backward)
        sent_ahead = got_ahead + pick(ahead, 2 * size - 2 - step)
        sent_behind = got_behind + pick(behind, 2 + step)
    return jnp.concatenate([sent_ahead, sent_behind], axis=1)


def reduce_share(stacked, groups, members):
    cores, xs = 2, 4
    zs = groups // (cores * xs)
    rows, width = stacked.shape[1:]
    index = lax.axis_index("seq")
    core = index % cores
    x_at = (index // cores) % xs
    z_at = index // (cores * xs)
    blocks = stacked.reshape(zs, xs, cores, rows, width)
    keep = lax.dynamic_index_in_dim(blocks, core, 2, keepdims=False)
    send = lax.dynamic_index_in_dim(blocks, 1 - core, 2, keepdims=False)
    summed = keep + lax.ppermute(send, "seq", seq_perm(groups, lambda i: i ^ 1))

    def x_move(step):
        def move(i):
            z, x, c = i // (cores * xs), (i // cores) % xs, i % cores
            return (z * xs + (x + step) % xs) * cores + c
        return seq_perm(groups, move)

    def z_move(step):
        def move(i):
            z, rest = i // (cores * xs), i % (cores * xs)
            return ((z + step) % zs) * cores * xs + rest
        return seq_perm(groups, move)

    by_x = jnp.swapaxes(summed, 0, 1)
    summed = ring_reduce(by_x, x_at, xs, x_move(1), x_move(xs - 1))
    summed = ring_reduce(summed[:, None], z_at, zs, z_move(1), z_move(zs - 1))[0]
    member = lax.axis_index("dp")
    bit = 1
    while bit < members:
        pairs = [(i, i ^ bit) for i in range(members)]
        summed = summed + lax.ppermute(summed, "dp", pairs)
        bit *= 2
    return summed


def solution(mesh):
    return jax.shard_map(
        shards,
        mesh=mesh,
        in_specs=(
            P("dp", None, "seq", None),
            P("dp", None, "seq"),
            P(),
            P(),
            P(),
            P(),
            P(),
            P(),
            P("dp", None, "seq", None),
        ),
        out_specs=(P("dp", None, "seq", None), P("seq", None), P("seq", None)),
        check_vma=False,
    )
```

```python
import math

import jax
import jax.numpy as jnp
from jax import lax
from jax.sharding import PartitionSpec as P

P_SIZE = 128
HEADS = 8
HEAD_DIM = 64
EB = 64
TB = 16


NORM_EPS = 1e-05


def normed_input(tokens, patch_mask, mask_token, gain):
    masked = jnp.where(patch_mask[..., None] == 1, mask_token, tokens.astype(jnp.float32))
    row_mean = jnp.mean(masked, axis=-1, keepdims=True)
    centred = masked - row_mean
    spread = jnp.mean(centred * centred, axis=-1, keepdims=True)
    normed = (centred * lax.rsqrt(spread + NORM_EPS) * gain).astype(jnp.bfloat16)
    return (masked, normed)


def forward_attend(queries, key_rows, values, allowed, factor):
    scores = (
        jnp.einsum("anhd,amhd->ahnm", queries, key_rows, preferred_element_type=jnp.float32)
        * factor
    )
    exponent = jnp.exp(scores) * allowed
    weights = exponent / jnp.sum(exponent, axis=-1, keepdims=True)
    rounded = weights.astype(jnp.bfloat16)
    output = jnp.einsum(
        "ahnm,amhd->anhd", rounded, values, preferred_element_type=jnp.float32
    ).astype(jnp.bfloat16)
    return (output, weights, rounded)


def backward_attend(queries, key_rows, values, weights, rounded, grad_out, factor):
    grad_values = jnp.einsum(
        "ahnm,anhd->amhd", rounded, grad_out, preferred_element_type=jnp.float32
    ).astype(jnp.bfloat16)
    grad_weights = jnp.einsum(
        "anhd,amhd->ahnm", grad_out, values, preferred_element_type=jnp.float32
    )
    inner_sum = jnp.sum(grad_weights * weights, axis=-1, keepdims=True)
    grad_scores = (weights * (grad_weights - inner_sum)).astype(jnp.bfloat16)
    grad_queries = (
        jnp.einsum("ahnm,amhd->anhd", grad_scores, key_rows, preferred_element_type=jnp.float32)
        * factor
    ).astype(jnp.bfloat16)
    grad_keys = (
        jnp.einsum("ahnm,anhd->amhd", grad_scores, queries, preferred_element_type=jnp.float32)
        * factor
    ).astype(jnp.bfloat16)
    return (grad_queries, grad_keys, grad_values)


def to_blocks(tensor, block_order, block_size):
    record_count, electrodes, local_patches = tensor.shape[:3]
    trailing = tensor.shape[3:]
    picked = jnp.take(tensor, block_order, axis=1)
    picked = picked.reshape(
        (record_count, electrodes // block_size, block_size, local_patches) + trailing
    )
    picked = jnp.moveaxis(picked, 3, 2)
    return picked.reshape(
        (record_count * (electrodes // block_size) * local_patches, block_size) + trailing
    )


def from_blocks(tensor, inverse, record_count, electrodes, local_patches):
    block_size = tensor.shape[1]
    trailing = tensor.shape[2:]
    restored = tensor.reshape(
        (record_count, electrodes // block_size, local_patches, block_size) + trailing
    )
    restored = jnp.moveaxis(restored, 2, 3).reshape(
        (record_count, electrodes, local_patches) + trailing
    )
    return jnp.take(restored, inverse, axis=1)


def shards(tokens, patch_mask, mask_token, gain, w_qkv, w_out, block_ids, temporal_mask, cotangent):
    record_count, electrodes, local_patches, model_width = tokens.shape
    half_width = model_width // 2
    heads_half = HEADS // 2
    factor = HEAD_DIM ** (-0.5)
    onehot = (jnp.arange(P_SIZE)[:, None] // TB == jnp.arange(P_SIZE // TB)[None, :]).astype(
        jnp.float32
    )
    time_allowed = jnp.dot(jnp.dot(onehot, temporal_mask.astype(jnp.float32)), onehot.T)
    same_block = (block_ids[:, None] == block_ids[None, :]).astype(jnp.float32)
    masked, normed = normed_input(tokens, patch_mask, mask_token, gain)
    normed_flat = normed.reshape(-1, model_width)
    local_columns = 3 * model_width
    projected = jnp.dot(normed_flat, w_qkv, preferred_element_type=jnp.float32).astype(jnp.bfloat16)
    projected = projected.reshape(
        record_count, electrodes, local_patches, local_columns // half_width, heads_half, HEAD_DIM
    )
    spatial = jnp.transpose(projected[0, :, :, :3], (1, 0, 2, 3, 4))
    space_out, space_weights, space_rounded = forward_attend(
        spatial[:, :, 0], spatial[:, :, 1], spatial[:, :, 2], same_block, factor
    )
    time_part = projected[:, :, :, 3:].reshape(
        record_count, electrodes, local_patches, 3 * half_width
    )
    regrouped = lax.all_to_all(time_part, SEQ, split_axis=1, concat_axis=2, tiled=True)
    items = regrouped.shape[0]
    owned = regrouped.shape[1]
    split_heads = regrouped.reshape(items * owned, P_SIZE, 3, heads_half, HEAD_DIM)
    time_out, time_weights, time_rounded = forward_attend(
        split_heads[:, :, 0], split_heads[:, :, 1], split_heads[:, :, 2], time_allowed, factor
    )
    time_out = time_out.reshape(items, owned, P_SIZE, half_width)
    time_back = lax.all_to_all(time_out, SEQ, split_axis=2, concat_axis=1, tiled=True)
    space_back = jnp.transpose(space_out, (1, 0, 2, 3)).reshape(
        record_count, electrodes, local_patches, half_width
    )
    attended = jnp.concatenate([space_back, time_back], axis=-1)
    attended_flat = attended.reshape(-1, model_width)
    layer_out = (
        masked.reshape(-1, model_width)
        + jnp.dot(attended_flat, w_out, preferred_element_type=jnp.float32)
    ).astype(jnp.bfloat16)
    layer_out = layer_out.reshape(tokens.shape)
    cot_flat = cotangent.reshape(-1, model_width)
    out_grad = jnp.einsum("tc,td->cd", cot_flat, attended_flat, preferred_element_type=jnp.float32)
    attended_grad = jnp.einsum(
        "td,cd->tc", cot_flat, w_out, preferred_element_type=jnp.float32
    ).astype(jnp.bfloat16)
    attended_grad = attended_grad.reshape(record_count, electrodes, local_patches, model_width)
    space_grad = jnp.transpose(
        attended_grad[0, :, :, :half_width].reshape(electrodes, local_patches, heads_half, HEAD_DIM),
        (1, 0, 2, 3),
    )
    space_grads = backward_attend(
        spatial[:, :, 0],
        spatial[:, :, 1],
        spatial[:, :, 2],
        space_weights,
        space_rounded,
        space_grad,
        factor,
    )
    spatial_grad = jnp.transpose(jnp.stack(space_grads, axis=2), (1, 0, 2, 3, 4))
    spatial_grad = spatial_grad.reshape(-1, 3 * half_width)
    time_grad = lax.all_to_all(
        attended_grad[..., half_width:], SEQ, split_axis=1, concat_axis=2, tiled=True
    )
    owned = time_grad.shape[1]
    split_heads = regrouped.reshape(record_count * owned, P_SIZE, 3, heads_half, HEAD_DIM)
    unused_out, time_weights, time_rounded = forward_attend(
        split_heads[:, :, 0], split_heads[:, :, 1], split_heads[:, :, 2], time_allowed, factor
    )
    time_grads = backward_attend(
        split_heads[:, :, 0],
        split_heads[:, :, 1],
        split_heads[:, :, 2],
        time_weights,
        time_rounded,
        time_grad.reshape(record_count * owned, P_SIZE, heads_half, HEAD_DIM),
        factor,
    )
    temporal_grad = jnp.stack(time_grads, axis=2).reshape(
        record_count, owned, P_SIZE, 3 * half_width
    )
    temporal_back = lax.all_to_all(
        temporal_grad, SEQ, split_axis=2, concat_axis=1, tiled=True
    ).reshape(-1, 3 * half_width)
    projected_grad = jnp.concatenate([spatial_grad, temporal_back], axis=1)
    qkv_grad = jnp.einsum(
        "tc,td->cd", projected_grad, normed_flat, preferred_element_type=jnp.float32
    )
    groups = lax.axis_size(SEQ)
    grad_scale = 1.0 / math.sqrt(
        record_count * lax.axis_size("dp") * electrodes * local_patches * groups
    )
    rows_qkv = qkv_grad.shape[0] // groups
    rows_out = model_width // groups
    stacked = jnp.concatenate(
        [
            qkv_grad.reshape(groups, rows_qkv, model_width),
            out_grad.reshape(groups, rows_out, model_width),
        ],
        axis=1,
    )
    share = reduce_share(stacked, groups, lax.axis_size("dp"))
    return (layer_out, share[:rows_qkv] * grad_scale, share[rows_qkv:] * grad_scale)


def reduce_share(stacked, groups, members):
    cores, xs = lax.axis_size("core"), lax.axis_size("x")
    zs = groups // (cores * xs)
    rows, width = stacked.shape[1:]
    core = lax.axis_index("core")
    blocks = stacked.reshape(zs, xs, cores, rows, width)
    keep = lax.dynamic_index_in_dim(blocks, core, 2, keepdims=False)
    send = lax.dynamic_index_in_dim(blocks, 1 - core, 2, keepdims=False)
    summed = keep + lax.ppermute(send, "core", [(0, 1), (1, 0)])
    summed = jnp.sum(lax.all_to_all(summed, "x", split_axis=1, concat_axis=1, tiled=True), axis=1)
    summed = jnp.sum(lax.all_to_all(summed, "zh", split_axis=0, concat_axis=0, tiled=True), axis=0)
    bit = 1
    while bit < members:
        pairs = [(i, i ^ bit) for i in range(members)]
        summed = summed + lax.ppermute(summed, "dp", pairs)
        bit *= 2
    return summed


SEQ = ("zh", "x", "core")


def solution(mesh):
    dp_size, seq_size = mesh.devices.shape
    split = jax.sharding.Mesh(
        mesh.devices.reshape(dp_size, seq_size // 8, 4, 2), ("dp",) + SEQ
    )
    return jax.shard_map(
        shards,
        mesh=split,
        in_specs=(
            P("dp", None, SEQ, None),
            P("dp", None, SEQ),
            P(),
            P(),
            P(),
            P(),
            P(),
            P(),
            P("dp", None, SEQ, None),
        ),
        out_specs=(P("dp", None, SEQ, None), P(SEQ, None), P(SEQ, None)),
        check_vma=False,
    )
```

```python
import math

import jax
import jax.numpy as jnp
from jax import lax
from jax.sharding import PartitionSpec as P

P_SIZE = 128
HEADS = 8
HEAD_DIM = 64
EB = 64
TB = 16


NORM_EPS = 1e-05


def normed_input(tokens, patch_mask, mask_token, gain):
    masked = jnp.where(patch_mask[..., None] == 1, mask_token, tokens.astype(jnp.float32))
    row_mean = jnp.mean(masked, axis=-1, keepdims=True)
    centred = masked - row_mean
    spread = jnp.mean(centred * centred, axis=-1, keepdims=True)
    normed = (centred * lax.rsqrt(spread + NORM_EPS) * gain).astype(jnp.bfloat16)
    return (masked, normed)


def forward_attend(queries, key_rows, values, allowed, factor):
    scores = (
        jnp.einsum("anhd,amhd->ahnm", queries, key_rows, preferred_element_type=jnp.float32)
        * factor
    )
    exponent = jnp.exp(scores) * allowed
    weights = exponent / jnp.sum(exponent, axis=-1, keepdims=True)
    rounded = weights.astype(jnp.bfloat16)
    output = jnp.einsum(
        "ahnm,amhd->anhd", rounded, values, preferred_element_type=jnp.float32
    ).astype(jnp.bfloat16)
    return (output, weights, rounded)


def backward_attend(queries, key_rows, values, weights, rounded, grad_out, factor):
    grad_values = jnp.einsum(
        "ahnm,anhd->amhd", rounded, grad_out, preferred_element_type=jnp.float32
    ).astype(jnp.bfloat16)
    grad_weights = jnp.einsum(
        "anhd,amhd->ahnm", grad_out, values, preferred_element_type=jnp.float32
    )
    inner_sum = jnp.sum(grad_weights * weights, axis=-1, keepdims=True)
    grad_scores = (weights * (grad_weights - inner_sum)).astype(jnp.bfloat16)
    grad_queries = (
        jnp.einsum("ahnm,amhd->anhd", grad_scores, key_rows, preferred_element_type=jnp.float32)
        * factor
    ).astype(jnp.bfloat16)
    grad_keys = (
        jnp.einsum("ahnm,anhd->amhd", grad_scores, queries, preferred_element_type=jnp.float32)
        * factor
    ).astype(jnp.bfloat16)
    return (grad_queries, grad_keys, grad_values)


def to_blocks(tensor, block_order, block_size):
    record_count, electrodes, local_patches = tensor.shape[:3]
    trailing = tensor.shape[3:]
    picked = jnp.take(tensor, block_order, axis=1)
    picked = picked.reshape(
        (record_count, electrodes // block_size, block_size, local_patches) + trailing
    )
    picked = jnp.moveaxis(picked, 3, 2)
    return picked.reshape(
        (record_count * (electrodes // block_size) * local_patches, block_size) + trailing
    )


def from_blocks(tensor, inverse, record_count, electrodes, local_patches):
    block_size = tensor.shape[1]
    trailing = tensor.shape[2:]
    restored = tensor.reshape(
        (record_count, electrodes // block_size, local_patches, block_size) + trailing
    )
    restored = jnp.moveaxis(restored, 2, 3).reshape(
        (record_count, electrodes, local_patches) + trailing
    )
    return jnp.take(restored, inverse, axis=1)


def shards(tokens, patch_mask, mask_token, gain, w_qkv, w_out, block_ids, temporal_mask, cotangent):
    record_count, electrodes, local_patches, model_width = tokens.shape
    half_width = model_width // 2
    heads_half = HEADS // 2
    factor = HEAD_DIM ** (-0.5)
    onehot = (jnp.arange(P_SIZE)[:, None] // TB == jnp.arange(P_SIZE // TB)[None, :]).astype(
        jnp.float32
    )
    time_allowed = jnp.dot(jnp.dot(onehot, temporal_mask.astype(jnp.float32)), onehot.T)
    same_block = (block_ids[:, None] == block_ids[None, :]).astype(jnp.float32)
    masked, normed = normed_input(tokens, patch_mask, mask_token, gain)
    normed_flat = normed.reshape(-1, model_width)
    local_columns = 3 * model_width
    projected = jnp.dot(normed_flat, w_qkv, preferred_element_type=jnp.float32).astype(jnp.bfloat16)
    projected = projected.reshape(
        record_count, electrodes, local_patches, local_columns // half_width, heads_half, HEAD_DIM
    )
    spatial = jnp.transpose(projected[0, :, :, :3], (1, 0, 2, 3, 4))
    space_out, space_weights, space_rounded = forward_attend(
        spatial[:, :, 0], spatial[:, :, 1], spatial[:, :, 2], same_block, factor
    )
    time_part = projected[:, :, :, 3:].reshape(
        record_count, electrodes, local_patches, 3 * half_width
    )
    regrouped = lax.all_to_all(time_part, "seq", split_axis=1, concat_axis=2, tiled=True)
    items = regrouped.shape[0]
    owned = regrouped.shape[1]
    split_heads = regrouped.reshape(items * owned, P_SIZE, 3, heads_half, HEAD_DIM)
    time_out, time_weights, time_rounded = forward_attend(
        split_heads[:, :, 0], split_heads[:, :, 1], split_heads[:, :, 2], time_allowed, factor
    )
    time_out = time_out.reshape(items, owned, P_SIZE, half_width)
    time_back = lax.all_to_all(time_out, "seq", split_axis=2, concat_axis=1, tiled=True)
    space_back = jnp.transpose(space_out, (1, 0, 2, 3)).reshape(
        record_count, electrodes, local_patches, half_width
    )
    attended = jnp.concatenate([space_back, time_back], axis=-1)
    attended_flat = attended.reshape(-1, model_width)
    layer_out = (
        masked.reshape(-1, model_width)
        + jnp.dot(attended_flat, w_out, preferred_element_type=jnp.float32)
    ).astype(jnp.bfloat16)
    layer_out = layer_out.reshape(tokens.shape)
    cot_flat = cotangent.reshape(-1, model_width)
    out_grad = jnp.einsum("tc,td->cd", cot_flat, attended_flat, preferred_element_type=jnp.float32)
    attended_grad = jnp.einsum(
        "td,cd->tc", cot_flat, w_out, preferred_element_type=jnp.float32
    ).astype(jnp.bfloat16)
    attended_grad = attended_grad.reshape(record_count, electrodes, local_patches, model_width)
    space_grad = jnp.transpose(
        attended_grad[0, :, :, :half_width].reshape(electrodes, local_patches, heads_half, HEAD_DIM),
        (1, 0, 2, 3),
    )
    space_grads = backward_attend(
        spatial[:, :, 0],
        spatial[:, :, 1],
        spatial[:, :, 2],
        space_weights,
        space_rounded,
        space_grad,
        factor,
    )
    spatial_grad = jnp.transpose(jnp.stack(space_grads, axis=2), (1, 0, 2, 3, 4))
    spatial_grad = spatial_grad.reshape(-1, 3 * half_width)
    time_grad = lax.all_to_all(
        attended_grad[..., half_width:], "seq", split_axis=1, concat_axis=2, tiled=True
    )
    owned = time_grad.shape[1]
    split_heads = regrouped.reshape(record_count * owned, P_SIZE, 3, heads_half, HEAD_DIM)
    unused_out, time_weights, time_rounded = forward_attend(
        split_heads[:, :, 0], split_heads[:, :, 1], split_heads[:, :, 2], time_allowed, factor
    )
    time_grads = backward_attend(
        split_heads[:, :, 0],
        split_heads[:, :, 1],
        split_heads[:, :, 2],
        time_weights,
        time_rounded,
        time_grad.reshape(record_count * owned, P_SIZE, heads_half, HEAD_DIM),
        factor,
    )
    temporal_grad = jnp.stack(time_grads, axis=2).reshape(
        record_count, owned, P_SIZE, 3 * half_width
    )
    temporal_back = lax.all_to_all(
        temporal_grad, "seq", split_axis=2, concat_axis=1, tiled=True
    ).reshape(-1, 3 * half_width)
    projected_grad = jnp.concatenate([spatial_grad, temporal_back], axis=1)
    qkv_grad = jnp.einsum(
        "tc,td->cd", projected_grad, normed_flat, preferred_element_type=jnp.float32
    )
    groups = lax.axis_size("seq")
    grad_scale = 1.0 / math.sqrt(
        record_count * lax.axis_size("dp") * electrodes * local_patches * groups
    )
    rows_qkv = qkv_grad.shape[0] // groups
    rows_out = model_width // groups
    stacked = jnp.concatenate(
        [
            qkv_grad.reshape(groups, rows_qkv, model_width),
            out_grad.reshape(groups, rows_out, model_width),
        ],
        axis=1,
    )
    share = reduce_share(stacked, groups, lax.axis_size("dp"))
    return (layer_out, share[:rows_qkv] * grad_scale, share[rows_qkv:] * grad_scale)


def seq_perm(groups, move):
    return [(index, move(index)) for index in range(groups)]


def ring_reduce(own, position, size, forward, backward):
    half = own.shape[2] // 2
    ahead, behind = own[:, :, :half], own[:, :, half:]

    def pick(values, offset):
        return lax.dynamic_index_in_dim(values, (position + offset) % size, 0, keepdims=False)

    sent_ahead = pick(ahead, size - 1)
    sent_behind = pick(behind, 1)
    for step in range(size - 1):
        got_ahead = lax.ppermute(sent_ahead.astype(jnp.bfloat16), "seq", forward)
        got_behind = lax.ppermute(sent_behind.astype(jnp.bfloat16), "seq", backward)
        sent_ahead = got_ahead.astype(jnp.float32) + pick(ahead, 2 * size - 2 - step)
        sent_behind = got_behind.astype(jnp.float32) + pick(behind, 2 + step)
    return jnp.concatenate([sent_ahead, sent_behind], axis=1)


def reduce_share(stacked, groups, members):
    cores, xs = 2, 4
    zs = groups // (cores * xs)
    rows, width = stacked.shape[1:]
    index = lax.axis_index("seq")
    core = index % cores
    x_at = (index // cores) % xs
    z_at = index // (cores * xs)
    blocks = stacked.reshape(zs, xs, cores, rows, width)
    keep = lax.dynamic_index_in_dim(blocks, core, 2, keepdims=False)
    send = lax.dynamic_index_in_dim(blocks, 1 - core, 2, keepdims=False)
    swapped = lax.ppermute(send.astype(jnp.bfloat16), "seq", seq_perm(groups, lambda i: i ^ 1))
    summed = keep + swapped.astype(jnp.float32)

    def x_move(step):
        def move(i):
            z, x, c = i // (cores * xs), (i // cores) % xs, i % cores
            return (z * xs + (x + step) % xs) * cores + c
        return seq_perm(groups, move)

    def z_move(step):
        def move(i):
            z, rest = i // (cores * xs), i % (cores * xs)
            return ((z + step) % zs) * cores * xs + rest
        return seq_perm(groups, move)

    by_x = jnp.swapaxes(summed, 0, 1)
    summed = ring_reduce(by_x, x_at, xs, x_move(1), x_move(xs - 1))
    summed = ring_reduce(summed[:, None], z_at, zs, z_move(1), z_move(zs - 1))[0]
    member = lax.axis_index("dp")
    bit = 1
    while bit < members:
        pairs = [(i, i ^ bit) for i in range(members)]
        summed = summed + lax.ppermute(summed, "dp", pairs)
        bit *= 2
    return summed


def solution(mesh):
    return jax.shard_map(
        shards,
        mesh=mesh,
        in_specs=(
            P("dp", None, "seq", None),
            P("dp", None, "seq"),
            P(),
            P(),
            P(),
            P(),
            P(),
            P(),
            P("dp", None, "seq", None),
        ),
        out_specs=(P("dp", None, "seq", None), P("seq", None), P("seq", None)),
        check_vma=False,
    )
```

```python
import math

import jax
import jax.numpy as jnp
from jax import lax
from jax.sharding import PartitionSpec as P

P_SIZE = 128
HEADS = 8
HEAD_DIM = 64
EB = 64
TB = 16


NORM_EPS = 1e-05


def normed_input(tokens, patch_mask, mask_token, gain):
    masked = jnp.where(patch_mask[..., None] == 1, mask_token, tokens.astype(jnp.float32))
    row_mean = jnp.mean(masked, axis=-1, keepdims=True)
    centred = masked - row_mean
    spread = jnp.mean(centred * centred, axis=-1, keepdims=True)
    normed = (centred * lax.rsqrt(spread + NORM_EPS) * gain).astype(jnp.bfloat16)
    return (masked, normed)


def forward_attend(queries, key_rows, values, allowed, factor):
    scores = (
        jnp.einsum("anhd,amhd->ahnm", queries, key_rows, preferred_element_type=jnp.float32)
        * factor
    )
    exponent = jnp.exp(scores) * allowed
    weights = exponent / jnp.sum(exponent, axis=-1, keepdims=True)
    rounded = weights.astype(jnp.bfloat16)
    output = jnp.einsum(
        "ahnm,amhd->anhd", rounded, values, preferred_element_type=jnp.float32
    ).astype(jnp.bfloat16)
    return (output, weights, rounded)


def backward_attend(queries, key_rows, values, weights, rounded, grad_out, factor):
    grad_values = jnp.einsum(
        "ahnm,anhd->amhd", rounded, grad_out, preferred_element_type=jnp.float32
    ).astype(jnp.bfloat16)
    grad_weights = jnp.einsum(
        "anhd,amhd->ahnm", grad_out, values, preferred_element_type=jnp.float32
    )
    inner_sum = jnp.sum(grad_weights * weights, axis=-1, keepdims=True)
    grad_scores = (weights * (grad_weights - inner_sum)).astype(jnp.bfloat16)
    grad_queries = (
        jnp.einsum("ahnm,amhd->anhd", grad_scores, key_rows, preferred_element_type=jnp.float32)
        * factor
    ).astype(jnp.bfloat16)
    grad_keys = (
        jnp.einsum("ahnm,anhd->amhd", grad_scores, queries, preferred_element_type=jnp.float32)
        * factor
    ).astype(jnp.bfloat16)
    return (grad_queries, grad_keys, grad_values)


def to_blocks(tensor, block_order, block_size):
    record_count, electrodes, local_patches = tensor.shape[:3]
    trailing = tensor.shape[3:]
    picked = jnp.take(tensor, block_order, axis=1)
    picked = picked.reshape(
        (record_count, electrodes // block_size, block_size, local_patches) + trailing
    )
    picked = jnp.moveaxis(picked, 3, 2)
    return picked.reshape(
        (record_count * (electrodes // block_size) * local_patches, block_size) + trailing
    )


def from_blocks(tensor, inverse, record_count, electrodes, local_patches):
    block_size = tensor.shape[1]
    trailing = tensor.shape[2:]
    restored = tensor.reshape(
        (record_count, electrodes // block_size, local_patches, block_size) + trailing
    )
    restored = jnp.moveaxis(restored, 2, 3).reshape(
        (record_count, electrodes, local_patches) + trailing
    )
    return jnp.take(restored, inverse, axis=1)


def shards(tokens, patch_mask, mask_token, gain, w_qkv, w_out, block_ids, temporal_mask, cotangent):
    record_count, electrodes, local_patches, model_width = tokens.shape
    half_width = model_width // 2
    heads_half = HEADS // 2
    factor = HEAD_DIM ** (-0.5)
    onehot = (jnp.arange(P_SIZE)[:, None] // TB == jnp.arange(P_SIZE // TB)[None, :]).astype(
        jnp.float32
    )
    time_allowed = jnp.dot(jnp.dot(onehot, temporal_mask.astype(jnp.float32)), onehot.T)
    same_block = (block_ids[:, None] == block_ids[None, :]).astype(jnp.float32)
    masked, normed = normed_input(tokens, patch_mask, mask_token, gain)
    normed_flat = normed.reshape(-1, model_width)
    group_columns = 3 * half_width
    time_part = jnp.dot(
        normed_flat, w_qkv[:, group_columns:], preferred_element_type=jnp.float32
    ).astype(jnp.bfloat16)
    time_part = time_part.reshape(record_count, electrodes, local_patches, group_columns)
    regrouped = lax.all_to_all(time_part, "seq", split_axis=1, concat_axis=2, tiled=True)
    projected = jnp.dot(
        normed_flat, w_qkv[:, :group_columns], preferred_element_type=jnp.float32
    ).astype(jnp.bfloat16)
    projected = projected.reshape(electrodes, local_patches, 3, heads_half, HEAD_DIM)
    spatial = jnp.transpose(projected, (1, 0, 2, 3, 4))
    space_out, space_weights, space_rounded = forward_attend(
        spatial[:, :, 0], spatial[:, :, 1], spatial[:, :, 2], same_block, factor
    )
    items = regrouped.shape[0]
    owned = regrouped.shape[1]
    split_heads = regrouped.reshape(items * owned, P_SIZE, 3, heads_half, HEAD_DIM)
    time_out, time_weights, time_rounded = forward_attend(
        split_heads[:, :, 0], split_heads[:, :, 1], split_heads[:, :, 2], time_allowed, factor
    )
    time_out = time_out.reshape(items, owned, P_SIZE, half_width)
    time_back = lax.all_to_all(time_out, "seq", split_axis=2, concat_axis=1, tiled=True)
    space_back = jnp.transpose(space_out, (1, 0, 2, 3)).reshape(
        record_count, electrodes, local_patches, half_width
    )
    attended = jnp.concatenate([space_back, time_back], axis=-1)
    attended_flat = attended.reshape(-1, model_width)
    layer_out = (
        masked.reshape(-1, model_width)
        + jnp.dot(attended_flat, w_out, preferred_element_type=jnp.float32)
    ).astype(jnp.bfloat16)
    layer_out = layer_out.reshape(tokens.shape)
    cot_flat = cotangent.reshape(-1, model_width)
    out_grad = jnp.einsum("tc,td->cd", cot_flat, attended_flat, preferred_element_type=jnp.float32)
    attended_grad = jnp.einsum(
        "td,cd->tc", cot_flat, w_out, preferred_element_type=jnp.float32
    ).astype(jnp.bfloat16)
    attended_grad = attended_grad.reshape(record_count, electrodes, local_patches, model_width)
    space_grad = jnp.transpose(
        attended_grad[0, :, :, :half_width].reshape(electrodes, local_patches, heads_half, HEAD_DIM),
        (1, 0, 2, 3),
    )
    space_grads = backward_attend(
        spatial[:, :, 0],
        spatial[:, :, 1],
        spatial[:, :, 2],
        space_weights,
        space_rounded,
        space_grad,
        factor,
    )
    spatial_grad = jnp.transpose(jnp.stack(space_grads, axis=2), (1, 0, 2, 3, 4))
    spatial_grad = spatial_grad.reshape(-1, 3 * half_width)
    time_grad = lax.all_to_all(
        attended_grad[..., half_width:], "seq", split_axis=1, concat_axis=2, tiled=True
    )
    owned = time_grad.shape[1]
    split_heads = regrouped.reshape(record_count * owned, P_SIZE, 3, heads_half, HEAD_DIM)
    unused_out, time_weights, time_rounded = forward_attend(
        split_heads[:, :, 0], split_heads[:, :, 1], split_heads[:, :, 2], time_allowed, factor
    )
    time_grads = backward_attend(
        split_heads[:, :, 0],
        split_heads[:, :, 1],
        split_heads[:, :, 2],
        time_weights,
        time_rounded,
        time_grad.reshape(record_count * owned, P_SIZE, heads_half, HEAD_DIM),
        factor,
    )
    temporal_grad = jnp.stack(time_grads, axis=2).reshape(
        record_count, owned, P_SIZE, 3 * half_width
    )
    temporal_back = lax.all_to_all(
        temporal_grad, "seq", split_axis=2, concat_axis=1, tiled=True
    ).reshape(-1, 3 * half_width)
    space_qkv_grad = jnp.einsum(
        "tc,td->cd", spatial_grad, normed_flat, preferred_element_type=jnp.float32
    )
    time_qkv_grad = jnp.einsum(
        "tc,td->cd", temporal_back, normed_flat, preferred_element_type=jnp.float32
    )
    qkv_grad = jnp.concatenate([space_qkv_grad, time_qkv_grad], axis=0)
    groups = lax.axis_size("seq")
    grad_scale = 1.0 / math.sqrt(
        record_count * lax.axis_size("dp") * electrodes * local_patches * groups
    )
    rows_qkv = qkv_grad.shape[0] // groups
    rows_out = model_width // groups
    stacked = jnp.concatenate(
        [
            qkv_grad.reshape(groups, rows_qkv, model_width),
            out_grad.reshape(groups, rows_out, model_width),
        ],
        axis=1,
    )
    share = reduce_share(stacked, groups, lax.axis_size("dp"))
    return (layer_out, share[:rows_qkv] * grad_scale, share[rows_qkv:] * grad_scale)


def seq_perm(groups, move):
    return [(index, move(index)) for index in range(groups)]


def ring_reduce(own, position, size, forward, backward):
    half = own.shape[2] // 2
    ahead, behind = own[:, :, :half], own[:, :, half:]

    def pick(values, offset):
        return lax.dynamic_index_in_dim(values, (position + offset) % size, 0, keepdims=False)

    sent_ahead = pick(ahead, size - 1)
    sent_behind = pick(behind, 1)
    for step in range(size - 1):
        got_ahead = lax.ppermute(sent_ahead.astype(jnp.bfloat16), "seq", forward)
        got_behind = lax.ppermute(sent_behind.astype(jnp.bfloat16), "seq", backward)
        sent_ahead = got_ahead.astype(jnp.float32) + pick(ahead, 2 * size - 2 - step)
        sent_behind = got_behind.astype(jnp.float32) + pick(behind, 2 + step)
    return jnp.concatenate([sent_ahead, sent_behind], axis=1)


def reduce_share(stacked, groups, members):
    cores, xs = 2, 4
    zs = groups // (cores * xs)
    rows, width = stacked.shape[1:]
    index = lax.axis_index("seq")
    core = index % cores
    x_at = (index // cores) % xs
    z_at = index // (cores * xs)
    blocks = stacked.reshape(zs, xs, cores, rows, width)
    keep = lax.dynamic_index_in_dim(blocks, core, 2, keepdims=False)
    send = lax.dynamic_index_in_dim(blocks, 1 - core, 2, keepdims=False)
    swapped = lax.ppermute(send.astype(jnp.bfloat16), "seq", seq_perm(groups, lambda i: i ^ 1))
    summed = keep + swapped.astype(jnp.float32)

    def x_move(step):
        def move(i):
            z, x, c = i // (cores * xs), (i // cores) % xs, i % cores
            return (z * xs + (x + step) % xs) * cores + c
        return seq_perm(groups, move)

    def z_move(step):
        def move(i):
            z, rest = i // (cores * xs), i % (cores * xs)
            return ((z + step) % zs) * cores * xs + rest
        return seq_perm(groups, move)

    by_x = jnp.swapaxes(summed, 0, 1)
    summed = ring_reduce(by_x, x_at, xs, x_move(1), x_move(xs - 1))
    summed = ring_reduce(summed[:, None], z_at, zs, z_move(1), z_move(zs - 1))[0]
    member = lax.axis_index("dp")
    bit = 1
    while bit < members:
        pairs = [(i, i ^ bit) for i in range(members)]
        summed = summed + lax.ppermute(summed, "dp", pairs)
        bit *= 2
    return summed


def solution(mesh):
    return jax.shard_map(
        shards,
        mesh=mesh,
        in_specs=(
            P("dp", None, "seq", None),
            P("dp", None, "seq"),
            P(),
            P(),
            P(),
            P(),
            P(),
            P(),
            P("dp", None, "seq", None),
        ),
        out_specs=(P("dp", None, "seq", None), P("seq", None), P("seq", None)),
        check_vma=False,
    )
```

```python
import math

import jax
import jax.numpy as jnp
from jax import lax
from jax.sharding import PartitionSpec as P

P_SIZE = 128
HEADS = 8
HEAD_DIM = 64
EB = 64
TB = 16


NORM_EPS = 1e-05


def normed_input(tokens, patch_mask, mask_token, gain):
    masked = jnp.where(patch_mask[..., None] == 1, mask_token, tokens.astype(jnp.float32))
    row_mean = jnp.mean(masked, axis=-1, keepdims=True)
    centred = masked - row_mean
    spread = jnp.mean(centred * centred, axis=-1, keepdims=True)
    normed = (centred * lax.rsqrt(spread + NORM_EPS) * gain).astype(jnp.bfloat16)
    return (masked, normed)


def forward_attend(queries, key_rows, values, allowed, factor):
    scores = (
        jnp.einsum("anhd,amhd->ahnm", queries, key_rows, preferred_element_type=jnp.float32)
        * factor
    )
    exponent = jnp.exp(scores) * allowed
    weights = exponent / jnp.sum(exponent, axis=-1, keepdims=True)
    rounded = weights.astype(jnp.bfloat16)
    output = jnp.einsum(
        "ahnm,amhd->anhd", rounded, values, preferred_element_type=jnp.float32
    ).astype(jnp.bfloat16)
    return (output, weights, rounded)


def backward_attend(queries, key_rows, values, weights, rounded, grad_out, factor):
    grad_values = jnp.einsum(
        "ahnm,anhd->amhd", rounded, grad_out, preferred_element_type=jnp.float32
    ).astype(jnp.bfloat16)
    grad_weights = jnp.einsum(
        "anhd,amhd->ahnm", grad_out, values, preferred_element_type=jnp.float32
    )
    inner_sum = jnp.sum(grad_weights * weights, axis=-1, keepdims=True)
    grad_scores = (weights * (grad_weights - inner_sum)).astype(jnp.bfloat16)
    grad_queries = (
        jnp.einsum("ahnm,amhd->anhd", grad_scores, key_rows, preferred_element_type=jnp.float32)
        * factor
    ).astype(jnp.bfloat16)
    grad_keys = (
        jnp.einsum("ahnm,anhd->amhd", grad_scores, queries, preferred_element_type=jnp.float32)
        * factor
    ).astype(jnp.bfloat16)
    return (grad_queries, grad_keys, grad_values)


def to_blocks(tensor, block_order, block_size):
    record_count, electrodes, local_patches = tensor.shape[:3]
    trailing = tensor.shape[3:]
    picked = jnp.take(tensor, block_order, axis=1)
    picked = picked.reshape(
        (record_count, electrodes // block_size, block_size, local_patches) + trailing
    )
    picked = jnp.moveaxis(picked, 3, 2)
    return picked.reshape(
        (record_count * (electrodes // block_size) * local_patches, block_size) + trailing
    )


def from_blocks(tensor, inverse, record_count, electrodes, local_patches):
    block_size = tensor.shape[1]
    trailing = tensor.shape[2:]
    restored = tensor.reshape(
        (record_count, electrodes // block_size, local_patches, block_size) + trailing
    )
    restored = jnp.moveaxis(restored, 2, 3).reshape(
        (record_count, electrodes, local_patches) + trailing
    )
    return jnp.take(restored, inverse, axis=1)


def shards(tokens, patch_mask, mask_token, gain, w_qkv, w_out, block_ids, temporal_mask, cotangent):
    record_count, electrodes, local_patches, model_width = tokens.shape
    half_width = model_width // 2
    heads_half = HEADS // 2
    factor = HEAD_DIM ** (-0.5)
    onehot = (jnp.arange(P_SIZE)[:, None] // TB == jnp.arange(P_SIZE // TB)[None, :]).astype(
        jnp.float32
    )
    time_allowed = jnp.dot(jnp.dot(onehot, temporal_mask.astype(jnp.float32)), onehot.T)
    same_block = (block_ids[:, None] == block_ids[None, :]).astype(jnp.float32)
    masked, normed = normed_input(tokens, patch_mask, mask_token, gain)
    normed_flat = normed.reshape(-1, model_width)
    group_columns = 3 * half_width
    time_part = jnp.dot(
        normed_flat, w_qkv[:, group_columns:], preferred_element_type=jnp.float32
    ).astype(jnp.bfloat16)
    time_part = time_part.reshape(record_count, electrodes, local_patches, group_columns)
    regrouped = lax.all_to_all(time_part, "seq", split_axis=1, concat_axis=2, tiled=True)
    projected = jnp.dot(
        normed_flat, w_qkv[:, :group_columns], preferred_element_type=jnp.float32
    ).astype(jnp.bfloat16)
    projected = projected.reshape(electrodes, local_patches, 3, heads_half, HEAD_DIM)
    spatial = jnp.transpose(projected, (1, 0, 2, 3, 4))
    space_out, space_weights, space_rounded = forward_attend(
        spatial[:, :, 0], spatial[:, :, 1], spatial[:, :, 2], same_block, factor
    )
    items = regrouped.shape[0]
    owned = regrouped.shape[1]
    split_heads = regrouped.reshape(items * owned, P_SIZE, 3, heads_half, HEAD_DIM)
    time_out, time_weights, time_rounded = forward_attend(
        split_heads[:, :, 0], split_heads[:, :, 1], split_heads[:, :, 2], time_allowed, factor
    )
    time_out = time_out.reshape(items, owned, P_SIZE, half_width)
    time_back = lax.all_to_all(time_out, "seq", split_axis=2, concat_axis=1, tiled=True)
    space_back = jnp.transpose(space_out, (1, 0, 2, 3)).reshape(
        record_count, electrodes, local_patches, half_width
    )
    attended = jnp.concatenate([space_back, time_back], axis=-1)
    attended_flat = attended.reshape(-1, model_width)
    layer_out = (
        masked.reshape(-1, model_width)
        + jnp.dot(attended_flat, w_out, preferred_element_type=jnp.float32)
    ).astype(jnp.bfloat16)
    layer_out = layer_out.reshape(tokens.shape)
    cot_flat = cotangent.reshape(-1, model_width)
    out_grad = jnp.einsum("tc,td->cd", cot_flat, attended_flat, preferred_element_type=jnp.float32)
    attended_grad = jnp.einsum(
        "td,cd->tc", cot_flat, w_out, preferred_element_type=jnp.float32
    ).astype(jnp.bfloat16)
    attended_grad = attended_grad.reshape(record_count, electrodes, local_patches, model_width)
    space_grad = jnp.transpose(
        attended_grad[0, :, :, :half_width].reshape(electrodes, local_patches, heads_half, HEAD_DIM),
        (1, 0, 2, 3),
    )
    space_grads = backward_attend(
        spatial[:, :, 0],
        spatial[:, :, 1],
        spatial[:, :, 2],
        space_weights,
        space_rounded,
        space_grad,
        factor,
    )
    spatial_grad = jnp.transpose(jnp.stack(space_grads, axis=2), (1, 0, 2, 3, 4))
    spatial_grad = spatial_grad.reshape(-1, 3 * half_width)
    time_grad = lax.all_to_all(
        attended_grad[..., half_width:], "seq", split_axis=1, concat_axis=2, tiled=True
    )
    owned = time_grad.shape[1]
    split_heads = regrouped.reshape(record_count * owned, P_SIZE, 3, heads_half, HEAD_DIM)
    unused_out, time_weights, time_rounded = forward_attend(
        split_heads[:, :, 0], split_heads[:, :, 1], split_heads[:, :, 2], time_allowed, factor
    )
    time_grads = backward_attend(
        split_heads[:, :, 0],
        split_heads[:, :, 1],
        split_heads[:, :, 2],
        time_weights,
        time_rounded,
        time_grad.reshape(record_count * owned, P_SIZE, heads_half, HEAD_DIM),
        factor,
    )
    temporal_grad = jnp.stack(time_grads, axis=2).reshape(
        record_count, owned, P_SIZE, 3 * half_width
    )
    temporal_back = lax.all_to_all(
        temporal_grad, "seq", split_axis=2, concat_axis=1, tiled=True
    ).reshape(-1, 3 * half_width)
    space_qkv_grad = jnp.einsum(
        "tc,td->cd", spatial_grad, normed_flat, preferred_element_type=jnp.float32
    )
    time_qkv_grad = jnp.einsum(
        "tc,td->cd", temporal_back, normed_flat, preferred_element_type=jnp.float32
    )
    qkv_grad = jnp.concatenate([space_qkv_grad, time_qkv_grad], axis=0)
    groups = lax.axis_size("seq")
    grad_scale = 1.0 / math.sqrt(
        record_count * lax.axis_size("dp") * electrodes * local_patches * groups
    )
    rows_qkv = qkv_grad.shape[0] // groups
    rows_out = model_width // groups
    stacked = jnp.concatenate(
        [
            qkv_grad.reshape(groups, rows_qkv, model_width),
            out_grad.reshape(groups, rows_out, model_width),
        ],
        axis=1,
    )
    share = reduce_share(stacked, groups, lax.axis_size("dp"))
    return (layer_out, share[:rows_qkv] * grad_scale, share[rows_qkv:] * grad_scale)


def seq_perm(groups, move):
    return [(index, move(index)) for index in range(groups)]


def ring_reduce(own, position, size, forward, backward):
    half = own.shape[2] // 2
    ahead, behind = own[:, :, :half], own[:, :, half:]

    def pick(values, offset):
        return lax.dynamic_index_in_dim(values, (position + offset) % size, 0, keepdims=False)

    sent_ahead = pick(ahead, size - 1)
    sent_behind = pick(behind, 1)
    for step in range(size - 1):
        got_ahead = lax.ppermute(sent_ahead.astype(jnp.bfloat16), "seq", forward)
        got_behind = lax.ppermute(sent_behind.astype(jnp.bfloat16), "seq", backward)
        sent_ahead = got_ahead.astype(jnp.float32) + pick(ahead, 2 * size - 2 - step)
        sent_behind = got_behind.astype(jnp.float32) + pick(behind, 2 + step)
    return jnp.concatenate([sent_ahead, sent_behind], axis=1)


def reduce_share(stacked, groups, members):
    cores, xs = 2, 4
    zs = groups // (cores * xs)
    rows, width = stacked.shape[1:]
    index = lax.axis_index("seq")
    core = index % cores
    x_at = (index // cores) % xs
    z_at = index // (cores * xs)
    blocks = stacked.reshape(zs, xs, cores, rows, width)
    keep = lax.dynamic_index_in_dim(blocks, core, 2, keepdims=False)
    send = lax.dynamic_index_in_dim(blocks, 1 - core, 2, keepdims=False)
    swapped = lax.ppermute(send.astype(jnp.bfloat16), "seq", seq_perm(groups, lambda i: i ^ 1))
    summed = keep + swapped.astype(jnp.float32)

    def x_move(step):
        def move(i):
            z, x, c = i // (cores * xs), (i // cores) % xs, i % cores
            return (z * xs + (x + step) % xs) * cores + c
        return seq_perm(groups, move)

    def z_move(step):
        def move(i):
            z, rest = i // (cores * xs), i % (cores * xs)
            return ((z + step) % zs) * cores * xs + rest
        return seq_perm(groups, move)

    by_x = jnp.swapaxes(summed, 0, 1)
    summed = ring_reduce(by_x, x_at, xs, x_move(1), x_move(xs - 1))
    summed = ring_reduce(summed[:, None], z_at, zs, z_move(1), z_move(zs - 1))[0]
    copies = jnp.broadcast_to(summed[None], (members,) + summed.shape)
    copies = lax.all_to_all(copies, "dp", split_axis=0, concat_axis=0, tiled=True)
    return jnp.sum(copies, axis=0)


def solution(mesh):
    return jax.shard_map(
        shards,
        mesh=mesh,
        in_specs=(
            P("dp", None, "seq", None),
            P("dp", None, "seq"),
            P(),
            P(),
            P(),
            P(),
            P(),
            P(),
            P("dp", None, "seq", None),
        ),
        out_specs=(P("dp", None, "seq", None), P("seq", None), P("seq", None)),
        check_vma=False,
    )
```

```python
import math

import jax
import jax.numpy as jnp
from jax import lax
from jax.sharding import PartitionSpec as P

P_SIZE = 128
HEADS = 8
HEAD_DIM = 64
EB = 64
TB = 16


NORM_EPS = 1e-05


def normed_input(tokens, patch_mask, mask_token, gain):
    masked = jnp.where(patch_mask[..., None] == 1, mask_token, tokens.astype(jnp.float32))
    row_mean = jnp.mean(masked, axis=-1, keepdims=True)
    centred = masked - row_mean
    spread = jnp.mean(centred * centred, axis=-1, keepdims=True)
    normed = (centred * lax.rsqrt(spread + NORM_EPS) * gain).astype(jnp.bfloat16)
    return (masked, normed)


def forward_attend(queries, key_rows, values, allowed, factor):
    scores = (
        jnp.einsum("anhd,amhd->ahnm", queries, key_rows, preferred_element_type=jnp.float32)
        * factor
    )
    exponent = jnp.exp(scores) * allowed
    weights = exponent / jnp.sum(exponent, axis=-1, keepdims=True)
    rounded = weights.astype(jnp.bfloat16)
    output = jnp.einsum(
        "ahnm,amhd->anhd", rounded, values, preferred_element_type=jnp.float32
    ).astype(jnp.bfloat16)
    return (output, weights, rounded)


def backward_attend(queries, key_rows, values, weights, rounded, grad_out, factor):
    grad_values = jnp.einsum(
        "ahnm,anhd->amhd", rounded, grad_out, preferred_element_type=jnp.float32
    ).astype(jnp.bfloat16)
    grad_weights = jnp.einsum(
        "anhd,amhd->ahnm", grad_out, values, preferred_element_type=jnp.float32
    )
    inner_sum = jnp.sum(grad_weights * weights, axis=-1, keepdims=True)
    grad_scores = (weights * (grad_weights - inner_sum)).astype(jnp.bfloat16)
    grad_queries = (
        jnp.einsum("ahnm,amhd->anhd", grad_scores, key_rows, preferred_element_type=jnp.float32)
        * factor
    ).astype(jnp.bfloat16)
    grad_keys = (
        jnp.einsum("ahnm,anhd->amhd", grad_scores, queries, preferred_element_type=jnp.float32)
        * factor
    ).astype(jnp.bfloat16)
    return (grad_queries, grad_keys, grad_values)


def to_blocks(tensor, block_order, block_size):
    record_count, electrodes, local_patches = tensor.shape[:3]
    trailing = tensor.shape[3:]
    picked = jnp.take(tensor, block_order, axis=1)
    picked = picked.reshape(
        (record_count, electrodes // block_size, block_size, local_patches) + trailing
    )
    picked = jnp.moveaxis(picked, 3, 2)
    return picked.reshape(
        (record_count * (electrodes // block_size) * local_patches, block_size) + trailing
    )


def from_blocks(tensor, inverse, record_count, electrodes, local_patches):
    block_size = tensor.shape[1]
    trailing = tensor.shape[2:]
    restored = tensor.reshape(
        (record_count, electrodes // block_size, local_patches, block_size) + trailing
    )
    restored = jnp.moveaxis(restored, 2, 3).reshape(
        (record_count, electrodes, local_patches) + trailing
    )
    return jnp.take(restored, inverse, axis=1)


def shards(tokens, patch_mask, mask_token, gain, w_qkv, w_out, block_ids, temporal_mask, cotangent):
    record_count, electrodes, local_patches, model_width = tokens.shape
    half_width = model_width // 2
    heads_half = HEADS // 2
    factor = HEAD_DIM ** (-0.5)
    onehot = (jnp.arange(P_SIZE)[:, None] // TB == jnp.arange(P_SIZE // TB)[None, :]).astype(
        jnp.float32
    )
    time_allowed = jnp.dot(jnp.dot(onehot, temporal_mask.astype(jnp.float32)), onehot.T)
    same_block = (block_ids[:, None] == block_ids[None, :]).astype(jnp.float32)
    masked, normed = normed_input(tokens, patch_mask, mask_token, gain)
    normed_flat = normed.reshape(-1, model_width)
    group_columns = 3 * half_width
    time_part = jnp.dot(
        normed_flat, w_qkv[:, group_columns:], preferred_element_type=jnp.float32
    ).astype(jnp.bfloat16)
    time_part = time_part.reshape(record_count, electrodes, local_patches, group_columns)
    regrouped = lax.all_to_all(time_part, SEQ, split_axis=1, concat_axis=2, tiled=True)
    projected = jnp.dot(
        normed_flat, w_qkv[:, :group_columns], preferred_element_type=jnp.float32
    ).astype(jnp.bfloat16)
    projected = projected.reshape(electrodes, local_patches, 3, heads_half, HEAD_DIM)
    spatial = jnp.transpose(projected, (1, 0, 2, 3, 4))
    space_out, space_weights, space_rounded = forward_attend(
        spatial[:, :, 0], spatial[:, :, 1], spatial[:, :, 2], same_block, factor
    )
    items = regrouped.shape[0]
    owned = regrouped.shape[1]
    split_heads = regrouped.reshape(items * owned, P_SIZE, 3, heads_half, HEAD_DIM)
    time_out, time_weights, time_rounded = forward_attend(
        split_heads[:, :, 0], split_heads[:, :, 1], split_heads[:, :, 2], time_allowed, factor
    )
    time_out = time_out.reshape(items, owned, P_SIZE, half_width)
    time_back = lax.all_to_all(time_out, SEQ, split_axis=2, concat_axis=1, tiled=True)
    space_back = jnp.transpose(space_out, (1, 0, 2, 3)).reshape(
        record_count, electrodes, local_patches, half_width
    )
    attended = jnp.concatenate([space_back, time_back], axis=-1)
    attended_flat = attended.reshape(-1, model_width)
    layer_out = (
        masked.reshape(-1, model_width)
        + jnp.dot(attended_flat, w_out, preferred_element_type=jnp.float32)
    ).astype(jnp.bfloat16)
    layer_out = layer_out.reshape(tokens.shape)
    cot_flat = cotangent.reshape(-1, model_width)
    out_grad = jnp.einsum("tc,td->cd", cot_flat, attended_flat, preferred_element_type=jnp.float32)
    attended_grad = jnp.einsum(
        "td,cd->tc", cot_flat, w_out, preferred_element_type=jnp.float32
    ).astype(jnp.bfloat16)
    attended_grad = attended_grad.reshape(record_count, electrodes, local_patches, model_width)
    space_grad = jnp.transpose(
        attended_grad[0, :, :, :half_width].reshape(electrodes, local_patches, heads_half, HEAD_DIM),
        (1, 0, 2, 3),
    )
    space_grads = backward_attend(
        spatial[:, :, 0],
        spatial[:, :, 1],
        spatial[:, :, 2],
        space_weights,
        space_rounded,
        space_grad,
        factor,
    )
    spatial_grad = jnp.transpose(jnp.stack(space_grads, axis=2), (1, 0, 2, 3, 4))
    spatial_grad = spatial_grad.reshape(-1, 3 * half_width)
    time_grad = lax.all_to_all(
        attended_grad[..., half_width:], SEQ, split_axis=1, concat_axis=2, tiled=True
    )
    owned = time_grad.shape[1]
    split_heads = regrouped.reshape(record_count * owned, P_SIZE, 3, heads_half, HEAD_DIM)
    unused_out, time_weights, time_rounded = forward_attend(
        split_heads[:, :, 0], split_heads[:, :, 1], split_heads[:, :, 2], time_allowed, factor
    )
    time_grads = backward_attend(
        split_heads[:, :, 0],
        split_heads[:, :, 1],
        split_heads[:, :, 2],
        time_weights,
        time_rounded,
        time_grad.reshape(record_count * owned, P_SIZE, heads_half, HEAD_DIM),
        factor,
    )
    temporal_grad = jnp.stack(time_grads, axis=2).reshape(
        record_count, owned, P_SIZE, 3 * half_width
    )
    temporal_back = lax.all_to_all(
        temporal_grad, SEQ, split_axis=2, concat_axis=1, tiled=True
    ).reshape(-1, 3 * half_width)
    space_qkv_grad = jnp.einsum(
        "tc,td->cd", spatial_grad, normed_flat, preferred_element_type=jnp.float32
    )
    time_qkv_grad = jnp.einsum(
        "tc,td->cd", temporal_back, normed_flat, preferred_element_type=jnp.float32
    )
    qkv_grad = jnp.concatenate([space_qkv_grad, time_qkv_grad], axis=0)
    groups = lax.axis_size(SEQ)
    grad_scale = 1.0 / math.sqrt(
        record_count * lax.axis_size("dp") * electrodes * local_patches * groups
    )
    rows_qkv = qkv_grad.shape[0] // groups
    rows_out = model_width // groups
    stacked = jnp.concatenate(
        [
            qkv_grad.reshape(groups, rows_qkv, model_width),
            out_grad.reshape(groups, rows_out, model_width),
        ],
        axis=1,
    )
    share = reduce_share(stacked, groups, lax.axis_size("dp"))
    return (layer_out, share[:rows_qkv] * grad_scale, share[rows_qkv:] * grad_scale)


def reduce_share(stacked, groups, members):
    cores = lax.axis_size("core")
    chips = groups // cores
    rows, width = stacked.shape[1:]
    core = lax.axis_index("core")
    blocks = stacked.reshape(chips, cores, rows, width)
    keep = lax.dynamic_index_in_dim(blocks, core, 1, keepdims=False)
    send = lax.dynamic_index_in_dim(blocks, 1 - core, 1, keepdims=False)
    swapped = lax.ppermute(send.astype(jnp.bfloat16), "core", [(0, 1), (1, 0)])
    summed = (keep + swapped.astype(jnp.float32)).astype(jnp.bfloat16)
    gathered = lax.all_to_all(summed, ("zh", "x"), split_axis=0, concat_axis=0, tiled=True)
    summed = jnp.sum(gathered.astype(jnp.float32), axis=0)
    bit = 1
    while bit < members:
        pairs = [(i, i ^ bit) for i in range(members)]
        summed = summed + lax.ppermute(summed, "dp", pairs)
        bit *= 2
    return summed


SEQ = ("zh", "x", "core")


def solution(mesh):
    dp_size, seq_size = mesh.devices.shape
    split = jax.sharding.Mesh(
        mesh.devices.reshape(dp_size, seq_size // 8, 4, 2), ("dp",) + SEQ
    )
    return jax.shard_map(
        shards,
        mesh=split,
        in_specs=(
            P("dp", None, SEQ, None),
            P("dp", None, SEQ),
            P(),
            P(),
            P(),
            P(),
            P(),
            P(),
            P("dp", None, SEQ, None),
        ),
        out_specs=(P("dp", None, SEQ, None), P(SEQ, None), P(SEQ, None)),
        check_vma=False,
    )
```

```python
import math

import jax
import jax.numpy as jnp
from jax import lax
from jax.sharding import PartitionSpec as P

P_SIZE = 128
HEADS = 8
HEAD_DIM = 64
EB = 64
TB = 16


NORM_EPS = 1e-05


def normed_input(tokens, patch_mask, mask_token, gain):
    masked = jnp.where(patch_mask[..., None] == 1, mask_token, tokens.astype(jnp.float32))
    row_mean = jnp.mean(masked, axis=-1, keepdims=True)
    centred = masked - row_mean
    spread = jnp.mean(centred * centred, axis=-1, keepdims=True)
    normed = (centred * lax.rsqrt(spread + NORM_EPS) * gain).astype(jnp.bfloat16)
    return (masked, normed)


def forward_attend(queries, key_rows, values, allowed, factor):
    scores = (
        jnp.einsum("anhd,amhd->ahnm", queries, key_rows, preferred_element_type=jnp.float32)
        * factor
    )
    exponent = jnp.exp(scores) * allowed
    weights = exponent / jnp.sum(exponent, axis=-1, keepdims=True)
    rounded = weights.astype(jnp.bfloat16)
    output = jnp.einsum(
        "ahnm,amhd->anhd", rounded, values, preferred_element_type=jnp.float32
    ).astype(jnp.bfloat16)
    return (output, weights, rounded)


def backward_attend(queries, key_rows, values, weights, rounded, grad_out, factor):
    grad_values = jnp.einsum(
        "ahnm,anhd->amhd", rounded, grad_out, preferred_element_type=jnp.float32
    ).astype(jnp.bfloat16)
    grad_weights = jnp.einsum(
        "anhd,amhd->ahnm", grad_out, values, preferred_element_type=jnp.float32
    )
    inner_sum = jnp.sum(grad_weights * weights, axis=-1, keepdims=True)
    grad_scores = (weights * (grad_weights - inner_sum)).astype(jnp.bfloat16)
    grad_queries = (
        jnp.einsum("ahnm,amhd->anhd", grad_scores, key_rows, preferred_element_type=jnp.float32)
        * factor
    ).astype(jnp.bfloat16)
    grad_keys = (
        jnp.einsum("ahnm,anhd->amhd", grad_scores, queries, preferred_element_type=jnp.float32)
        * factor
    ).astype(jnp.bfloat16)
    return (grad_queries, grad_keys, grad_values)


def to_blocks(tensor, block_order, block_size):
    record_count, electrodes, local_patches = tensor.shape[:3]
    trailing = tensor.shape[3:]
    picked = jnp.take(tensor, block_order, axis=1)
    picked = picked.reshape(
        (record_count, electrodes // block_size, block_size, local_patches) + trailing
    )
    picked = jnp.moveaxis(picked, 3, 2)
    return picked.reshape(
        (record_count * (electrodes // block_size) * local_patches, block_size) + trailing
    )


def from_blocks(tensor, inverse, record_count, electrodes, local_patches):
    block_size = tensor.shape[1]
    trailing = tensor.shape[2:]
    restored = tensor.reshape(
        (record_count, electrodes // block_size, local_patches, block_size) + trailing
    )
    restored = jnp.moveaxis(restored, 2, 3).reshape(
        (record_count, electrodes, local_patches) + trailing
    )
    return jnp.take(restored, inverse, axis=1)


def shards(tokens, patch_mask, mask_token, gain, w_qkv, w_out, block_ids, temporal_mask, cotangent):
    record_count, electrodes, local_patches, model_width = tokens.shape
    half_width = model_width // 2
    heads_half = HEADS // 2
    factor = HEAD_DIM ** (-0.5)
    onehot = (jnp.arange(P_SIZE)[:, None] // TB == jnp.arange(P_SIZE // TB)[None, :]).astype(
        jnp.float32
    )
    time_allowed = jnp.dot(jnp.dot(onehot, temporal_mask.astype(jnp.float32)), onehot.T)
    same_block = (block_ids[:, None] == block_ids[None, :]).astype(jnp.float32)
    masked, normed = normed_input(tokens, patch_mask, mask_token, gain)
    normed_flat = normed.reshape(-1, model_width)
    group_columns = 3 * half_width
    time_part = jnp.dot(
        normed_flat, w_qkv[:, group_columns:], preferred_element_type=jnp.float32
    ).astype(jnp.bfloat16)
    time_part = time_part.reshape(record_count, electrodes, local_patches, group_columns)
    regrouped = lax.all_to_all(time_part, SEQ, split_axis=1, concat_axis=2, tiled=True)
    projected = jnp.dot(
        normed_flat, w_qkv[:, :group_columns], preferred_element_type=jnp.float32
    ).astype(jnp.bfloat16)
    projected = projected.reshape(electrodes, local_patches, 3, heads_half, HEAD_DIM)
    spatial = jnp.transpose(projected, (1, 0, 2, 3, 4))
    space_out, space_weights, space_rounded = forward_attend(
        spatial[:, :, 0], spatial[:, :, 1], spatial[:, :, 2], same_block, factor
    )
    items = regrouped.shape[0]
    owned = regrouped.shape[1]
    split_heads = regrouped.reshape(items * owned, P_SIZE, 3, heads_half, HEAD_DIM)
    time_out, time_weights, time_rounded = forward_attend(
        split_heads[:, :, 0], split_heads[:, :, 1], split_heads[:, :, 2], time_allowed, factor
    )
    time_out = time_out.reshape(items, owned, P_SIZE, half_width)
    time_back = lax.all_to_all(time_out, SEQ, split_axis=2, concat_axis=1, tiled=True)
    space_back = jnp.transpose(space_out, (1, 0, 2, 3)).reshape(
        record_count, electrodes, local_patches, half_width
    )
    attended = jnp.concatenate([space_back, time_back], axis=-1)
    attended_flat = attended.reshape(-1, model_width)
    layer_out = (
        masked.reshape(-1, model_width)
        + jnp.dot(attended_flat, w_out, preferred_element_type=jnp.float32)
    ).astype(jnp.bfloat16)
    layer_out = layer_out.reshape(tokens.shape)
    cot_flat = cotangent.reshape(-1, model_width)
    out_grad = jnp.einsum("tc,td->cd", cot_flat, attended_flat, preferred_element_type=jnp.float32)
    attended_grad = jnp.einsum(
        "td,cd->tc", cot_flat, w_out, preferred_element_type=jnp.float32
    ).astype(jnp.bfloat16)
    attended_grad = attended_grad.reshape(record_count, electrodes, local_patches, model_width)
    space_grad = jnp.transpose(
        attended_grad[0, :, :, :half_width].reshape(electrodes, local_patches, heads_half, HEAD_DIM),
        (1, 0, 2, 3),
    )
    space_grads = backward_attend(
        spatial[:, :, 0],
        spatial[:, :, 1],
        spatial[:, :, 2],
        space_weights,
        space_rounded,
        space_grad,
        factor,
    )
    spatial_grad = jnp.transpose(jnp.stack(space_grads, axis=2), (1, 0, 2, 3, 4))
    spatial_grad = spatial_grad.reshape(-1, 3 * half_width)
    time_grad = lax.all_to_all(
        attended_grad[..., half_width:], SEQ, split_axis=1, concat_axis=2, tiled=True
    )
    owned = time_grad.shape[1]
    split_heads = regrouped.reshape(record_count * owned, P_SIZE, 3, heads_half, HEAD_DIM)
    unused_out, time_weights, time_rounded = forward_attend(
        split_heads[:, :, 0], split_heads[:, :, 1], split_heads[:, :, 2], time_allowed, factor
    )
    time_grads = backward_attend(
        split_heads[:, :, 0],
        split_heads[:, :, 1],
        split_heads[:, :, 2],
        time_weights,
        time_rounded,
        time_grad.reshape(record_count * owned, P_SIZE, heads_half, HEAD_DIM),
        factor,
    )
    temporal_grad = jnp.stack(time_grads, axis=2).reshape(
        record_count, owned, P_SIZE, 3 * half_width
    )
    temporal_back = lax.all_to_all(
        temporal_grad, SEQ, split_axis=2, concat_axis=1, tiled=True
    ).reshape(-1, 3 * half_width)
    space_qkv_grad = jnp.einsum(
        "tc,td->cd", spatial_grad, normed_flat, preferred_element_type=jnp.float32
    )
    time_qkv_grad = jnp.einsum(
        "tc,td->cd", temporal_back, normed_flat, preferred_element_type=jnp.float32
    )
    qkv_grad = jnp.concatenate([space_qkv_grad, time_qkv_grad], axis=0)
    groups = lax.axis_size(SEQ)
    grad_scale = 1.0 / math.sqrt(
        record_count * lax.axis_size(DP) * electrodes * local_patches * groups
    )
    rows_qkv = qkv_grad.shape[0] // groups
    rows_out = model_width // groups
    stacked = jnp.concatenate(
        [
            qkv_grad.reshape(groups, rows_qkv, model_width),
            out_grad.reshape(groups, rows_out, model_width),
        ],
        axis=1,
    )
    share = reduce_share(stacked, groups, lax.axis_size(DP))
    return (layer_out, share[:rows_qkv] * grad_scale, share[rows_qkv:] * grad_scale)


def reduce_share(stacked, groups, members):
    cores = lax.axis_size("core")
    chips = groups // cores
    rows, width = stacked.shape[1:]
    core = lax.axis_index("core")
    blocks = stacked.reshape(chips, cores, rows, width)
    keep = lax.dynamic_index_in_dim(blocks, core, 1, keepdims=False)
    send = lax.dynamic_index_in_dim(blocks, 1 - core, 1, keepdims=False)
    swapped = lax.ppermute(send.astype(jnp.bfloat16), "core", [(0, 1), (1, 0)])
    summed = (keep + swapped.astype(jnp.float32)).astype(jnp.bfloat16)
    gathered = lax.all_to_all(summed, ("zh", "x"), split_axis=0, concat_axis=0, tiled=True)
    summed = jnp.sum(gathered.astype(jnp.float32), axis=0)
    summed = summed + lax.ppermute(summed, "zl", [(0, 1), (1, 0)])
    ys = lax.axis_size("y")
    copies = jnp.broadcast_to(summed[None], (ys,) + summed.shape)
    copies = lax.all_to_all(copies, "y", split_axis=0, concat_axis=0, tiled=True)
    return jnp.sum(copies, axis=0)


SEQ = ("zh", "x", "core")
DP = ("y", "zl")


def solution(mesh):
    dp_size, seq_size = mesh.devices.shape
    split = jax.sharding.Mesh(
        mesh.devices.reshape(dp_size // 2, 2, seq_size // 8, 4, 2), DP + SEQ
    )
    return jax.shard_map(
        shards,
        mesh=split,
        in_specs=(
            P(DP, None, SEQ, None),
            P(DP, None, SEQ),
            P(),
            P(),
            P(),
            P(),
            P(),
            P(),
            P(DP, None, SEQ, None),
        ),
        out_specs=(P(DP, None, SEQ, None), P(SEQ, None), P(SEQ, None)),
        check_vma=False,
    )
```

```python
import math

import jax
import jax.numpy as jnp
from jax import lax
from jax.sharding import PartitionSpec as P

P_SIZE = 128
HEADS = 8
HEAD_DIM = 64
EB = 64
TB = 16


NORM_EPS = 1e-05


def normed_input(tokens, patch_mask, mask_token, gain):
    masked = jnp.where(patch_mask[..., None] == 1, mask_token, tokens.astype(jnp.float32))
    row_mean = jnp.mean(masked, axis=-1, keepdims=True)
    centred = masked - row_mean
    spread = jnp.mean(centred * centred, axis=-1, keepdims=True)
    normed = (centred * lax.rsqrt(spread + NORM_EPS) * gain).astype(jnp.bfloat16)
    return (masked, normed)


def forward_attend(queries, key_rows, values, allowed, factor):
    scores = (
        jnp.einsum("anhd,amhd->ahnm", queries, key_rows, preferred_element_type=jnp.float32)
        * factor
    )
    exponent = jnp.exp(scores) * allowed
    weights = exponent / jnp.sum(exponent, axis=-1, keepdims=True)
    rounded = weights.astype(jnp.bfloat16)
    output = jnp.einsum(
        "ahnm,amhd->anhd", rounded, values, preferred_element_type=jnp.float32
    ).astype(jnp.bfloat16)
    return (output, weights, rounded)


def backward_attend(queries, key_rows, values, weights, rounded, grad_out, factor):
    grad_values = jnp.einsum(
        "ahnm,anhd->amhd", rounded, grad_out, preferred_element_type=jnp.float32
    ).astype(jnp.bfloat16)
    grad_weights = jnp.einsum(
        "anhd,amhd->ahnm", grad_out, values, preferred_element_type=jnp.float32
    )
    inner_sum = jnp.sum(grad_weights * weights, axis=-1, keepdims=True)
    grad_scores = (weights * (grad_weights - inner_sum)).astype(jnp.bfloat16)
    grad_queries = (
        jnp.einsum("ahnm,amhd->anhd", grad_scores, key_rows, preferred_element_type=jnp.float32)
        * factor
    ).astype(jnp.bfloat16)
    grad_keys = (
        jnp.einsum("ahnm,anhd->amhd", grad_scores, queries, preferred_element_type=jnp.float32)
        * factor
    ).astype(jnp.bfloat16)
    return (grad_queries, grad_keys, grad_values)


def to_blocks(tensor, block_order, block_size):
    record_count, electrodes, local_patches = tensor.shape[:3]
    trailing = tensor.shape[3:]
    picked = jnp.take(tensor, block_order, axis=1)
    picked = picked.reshape(
        (record_count, electrodes // block_size, block_size, local_patches) + trailing
    )
    picked = jnp.moveaxis(picked, 3, 2)
    return picked.reshape(
        (record_count * (electrodes // block_size) * local_patches, block_size) + trailing
    )


def from_blocks(tensor, inverse, record_count, electrodes, local_patches):
    block_size = tensor.shape[1]
    trailing = tensor.shape[2:]
    restored = tensor.reshape(
        (record_count, electrodes // block_size, local_patches, block_size) + trailing
    )
    restored = jnp.moveaxis(restored, 2, 3).reshape(
        (record_count, electrodes, local_patches) + trailing
    )
    return jnp.take(restored, inverse, axis=1)


def shards(tokens, patch_mask, mask_token, gain, w_qkv, w_out, block_ids, temporal_mask, cotangent):
    record_count, electrodes, local_patches, model_width = tokens.shape
    half_width = model_width // 2
    heads_half = HEADS // 2
    factor = HEAD_DIM ** (-0.5)
    onehot = (jnp.arange(P_SIZE)[:, None] // TB == jnp.arange(P_SIZE // TB)[None, :]).astype(
        jnp.float32
    )
    time_allowed = jnp.dot(jnp.dot(onehot, temporal_mask.astype(jnp.float32)), onehot.T)
    same_block = (block_ids[:, None] == block_ids[None, :]).astype(jnp.float32)
    masked, normed = normed_input(tokens, patch_mask, mask_token, gain)
    normed_flat = normed.reshape(-1, model_width)
    group_columns = 3 * half_width
    time_part = jnp.dot(
        normed_flat, w_qkv[:, group_columns:], preferred_element_type=jnp.float32
    ).astype(jnp.bfloat16)
    time_part = time_part.reshape(record_count, electrodes, local_patches, group_columns)
    regrouped = lax.all_to_all(time_part, SEQ, split_axis=1, concat_axis=2, tiled=True)
    projected = jnp.dot(
        normed_flat, w_qkv[:, :group_columns], preferred_element_type=jnp.float32
    ).astype(jnp.bfloat16)
    projected = projected.reshape(electrodes, local_patches, 3, heads_half, HEAD_DIM)
    spatial = jnp.transpose(projected, (1, 0, 2, 3, 4))
    space_out, space_weights, space_rounded = forward_attend(
        spatial[:, :, 0], spatial[:, :, 1], spatial[:, :, 2], same_block, factor
    )
    items = regrouped.shape[0]
    owned = regrouped.shape[1]
    split_heads = regrouped.reshape(items * owned, P_SIZE, 3, heads_half, HEAD_DIM)
    time_out, time_weights, time_rounded = forward_attend(
        split_heads[:, :, 0], split_heads[:, :, 1], split_heads[:, :, 2], time_allowed, factor
    )
    time_out = time_out.reshape(items, owned, P_SIZE, half_width)
    time_back = lax.all_to_all(time_out, SEQ, split_axis=2, concat_axis=1, tiled=True)
    space_back = jnp.transpose(space_out, (1, 0, 2, 3)).reshape(
        record_count, electrodes, local_patches, half_width
    )
    attended = jnp.concatenate([space_back, time_back], axis=-1)
    attended_flat = attended.reshape(-1, model_width)
    layer_out = (
        masked.reshape(-1, model_width)
        + jnp.dot(attended_flat, w_out, preferred_element_type=jnp.float32)
    ).astype(jnp.bfloat16)
    layer_out = layer_out.reshape(tokens.shape)
    cot_flat = cotangent.reshape(-1, model_width)
    out_grad = jnp.einsum("tc,td->cd", cot_flat, attended_flat, preferred_element_type=jnp.float32)
    attended_grad = jnp.einsum(
        "td,cd->tc", cot_flat, w_out, preferred_element_type=jnp.float32
    ).astype(jnp.bfloat16)
    attended_grad = attended_grad.reshape(record_count, electrodes, local_patches, model_width)
    space_grad = jnp.transpose(
        attended_grad[0, :, :, :half_width].reshape(electrodes, local_patches, heads_half, HEAD_DIM),
        (1, 0, 2, 3),
    )
    space_grads = backward_attend(
        spatial[:, :, 0],
        spatial[:, :, 1],
        spatial[:, :, 2],
        space_weights,
        space_rounded,
        space_grad,
        factor,
    )
    spatial_grad = jnp.transpose(jnp.stack(space_grads, axis=2), (1, 0, 2, 3, 4))
    spatial_grad = spatial_grad.reshape(-1, 3 * half_width)
    time_grad = lax.all_to_all(
        attended_grad[..., half_width:], SEQ, split_axis=1, concat_axis=2, tiled=True
    )
    owned = time_grad.shape[1]
    split_heads = regrouped.reshape(record_count * owned, P_SIZE, 3, heads_half, HEAD_DIM)
    unused_out, time_weights, time_rounded = forward_attend(
        split_heads[:, :, 0], split_heads[:, :, 1], split_heads[:, :, 2], time_allowed, factor
    )
    time_grads = backward_attend(
        split_heads[:, :, 0],
        split_heads[:, :, 1],
        split_heads[:, :, 2],
        time_weights,
        time_rounded,
        time_grad.reshape(record_count * owned, P_SIZE, heads_half, HEAD_DIM),
        factor,
    )
    temporal_grad = jnp.stack(time_grads, axis=2).reshape(
        record_count, owned, P_SIZE, 3 * half_width
    )
    temporal_back = lax.all_to_all(
        temporal_grad, SEQ, split_axis=2, concat_axis=1, tiled=True
    ).reshape(-1, 3 * half_width)
    space_qkv_grad = jnp.einsum(
        "tc,td->cd", spatial_grad, normed_flat, preferred_element_type=jnp.float32
    )
    time_qkv_grad = jnp.einsum(
        "tc,td->cd", temporal_back, normed_flat, preferred_element_type=jnp.float32
    )
    qkv_grad = jnp.concatenate([space_qkv_grad, time_qkv_grad], axis=0)
    groups = lax.axis_size(SEQ)
    grad_scale = 1.0 / math.sqrt(
        record_count * lax.axis_size("dp") * electrodes * local_patches * groups
    )
    rows_qkv = qkv_grad.shape[0] // groups
    rows_out = model_width // groups
    qkv_share = reduce_share(qkv_grad.reshape(groups, rows_qkv, model_width), groups, lax.axis_size("dp"))
    out_share = reduce_share(out_grad.reshape(groups, rows_out, model_width), groups, lax.axis_size("dp"))
    return (layer_out, qkv_share * grad_scale, out_share * grad_scale)


def reduce_share(stacked, groups, members):
    cores = lax.axis_size("core")
    chips = groups // cores
    rows, width = stacked.shape[1:]
    core = lax.axis_index("core")
    blocks = stacked.reshape(chips, cores, rows, width)
    keep = lax.dynamic_index_in_dim(blocks, core, 1, keepdims=False)
    send = lax.dynamic_index_in_dim(blocks, 1 - core, 1, keepdims=False)
    swapped = lax.ppermute(send.astype(jnp.bfloat16), "core", [(0, 1), (1, 0)])
    summed = (keep + swapped.astype(jnp.float32)).astype(jnp.bfloat16)
    gathered = lax.all_to_all(summed, ("zh", "x"), split_axis=0, concat_axis=0, tiled=True)
    summed = jnp.sum(gathered.astype(jnp.float32), axis=0)
    bit = 1
    while bit < members:
        pairs = [(i, i ^ bit) for i in range(members)]
        summed = summed + lax.ppermute(summed, "dp", pairs)
        bit *= 2
    return summed


SEQ = ("zh", "x", "core")


def solution(mesh):
    dp_size, seq_size = mesh.devices.shape
    split = jax.sharding.Mesh(
        mesh.devices.reshape(dp_size, seq_size // 8, 4, 2), ("dp",) + SEQ
    )
    return jax.shard_map(
        shards,
        mesh=split,
        in_specs=(
            P("dp", None, SEQ, None),
            P("dp", None, SEQ),
            P(),
            P(),
            P(),
            P(),
            P(),
            P(),
            P("dp", None, SEQ, None),
        ),
        out_specs=(P("dp", None, SEQ, None), P(SEQ, None), P(SEQ, None)),
        check_vma=False,
    )
```
